256 devices in a mesh: samp: 64 (over x, z, core), chan: 4 (over y).
Axes of the slice: x: 4, y: 4, z: 8, core: 2. Of those that a mesh axis runs over, the one named last changes fastest.
Arguments:
- loads: float32 [256, 196608], P('chan', 'samp')
- coords: float32 [6, 196608], P(None, 'samp'), may hold values from -6 to 6
- coreg_factor: float32 [256, 256], P('chan'), may hold values from -0.375 to 0.375
- noise: float32 [256], P('chan'), may hold values from 0.1 to 1
- run_perm: int32 [196608], P('samp'), may hold values from 0 to 196607, as said below
- block_nbrs: int32 [1536, 12], P('samp'), may hold values from 0 to 1535, as said below
- nbr_count: int32 [1536], P('samp'), may hold values from 1 to 12, as said below
Outputs:
- solution: float32 [256, 196608], P('chan', 'samp')
- residual: float32 [256, 196608], P('chan', 'samp')
The draws below stay inside these ranges and needn't reach their ends.
Inputs may be any that keep to these rules, and one draw needn't show every extreme that they name: `block_nbrs`: the blocks are cut into clusters of consecutive blocks, each of 1 to 12 blocks. Row b lists the blocks of b's cluster in increasing order in its first nbr_count[b] entries; its other entries hold b itself. `nbr_count`: the size of block b's cluster; some block's cluster has 12 blocks. `run_perm`: within each aligned range of 3072 positions (the runs of one samp device), a permutation of that range.
All inputs are finite; a program needn't handle non-finite values.
Results may differ from the reference program's by a relative error of at most 0.0035.
Values may be sent and summed in bfloat16 or wider, within the bound.
No kernel may reach another device: no remote copies, remote signals or barrier semaphores. Data moves between devices by JAX's collectives and lax.ppermute only.
A program may use at most 64 MiB of HBM per device.

```python
import math
import jax
import jax.numpy as jnp
from jax import lax

CH = 256
DIM = 6
BS = 128
MAXC = 12
ITERS = 2
BLK_DEV = 24
NBLK = 1536
RUNS = 196608


def draw_loads(key, part):
    key_vals, key_rows, key_cols = jax.random.split(key, 3)
    position = jnp.arange(RUNS).astype(jnp.float32) / RUNS
    row_scale = jnp.exp(jax.random.uniform(key_rows, (RUNS,), jnp.float32, -1.2, 1.2))
    col_scale = jnp.exp(jax.random.uniform(key_cols, (CH,), jnp.float32, -1.2, 1.2))
    values = jax.random.normal(key_vals, (CH, RUNS), jnp.float32)
    trend = 0.6 + 1.2 * position
    return (values * col_scale[:, None] * (row_scale * trend)[None, :]).astype(jnp.float32)


def draw_run_perm(key, part):
    per_device = BLK_DEV * BS
    device_count = RUNS // per_device
    keys = jax.random.split(jax.random.fold_in(key, 5), device_count)
    perms = jax.vmap(lambda one_key: jax.random.permutation(one_key, per_device))(keys)
    shifted = perms + (jnp.arange(device_count) * per_device)[:, None]
    return shifted.reshape(-1).astype(jnp.int32)


def cluster_pattern(key):
    base = jax.random.fold_in(key, 11)
    key_level, key_len, key_phase = jax.random.split(base, 3)
    clusters = NBLK
    levels = jax.random.randint(key_level, (clusters // 16 + 1,), 1, 5)
    caps = jnp.maximum(1, MAXC * levels // 4)
    cap_each = jnp.repeat(caps, 16)[:clusters]
    raw = jax.random.randint(key_len, (clusters,), 0, 1 << 20)
    drawn = raw % cap_each + 1
    phase = jax.random.randint(key_phase, (), 0, 4)
    order = jnp.arange(clusters)
    drawn = jnp.where(order % 8 == phase, MAXC, drawn)
    ends = jnp.cumsum(drawn)
    blocks = jnp.arange(NBLK)
    cluster_of = jnp.sum((ends[None, :] <= blocks[:, None]).astype(jnp.int32), axis=1)
    begins = jnp.where(cluster_of > 0, ends[jnp.maximum(cluster_of - 1, 0)], 0)
    finish = jnp.minimum(ends[cluster_of], NBLK)
    counts = finish - begins
    slots = jnp.arange(MAXC)
    listed = jnp.where(slots[None, :] < counts[:, None], begins[:, None] + slots[None, :], blocks[:, None])
    return (listed.astype(jnp.int32), counts.astype(jnp.int32))


def draw_block_nbrs(key, part):
    return cluster_pattern(key)[0]


def draw_nbr_count(key, part):
    return cluster_pattern(key)[1]


def level_of(key, shape, shards, smallest, top_value):
    factor_of, own = 1.0, jax.random.fold_in(key, 6)
    for dim, parts in shards:
        draws = jnp.exp(jax.random.uniform(jax.random.fold_in(own, dim), (parts,), jnp.float32, smallest / len(shards), top_value / len(shards)))
        factor_of = factor_of * jnp.repeat(draws, shape[dim] // parts).reshape([-1 if axis == dim else 1 for axis in range(len(shape))])
    return factor_of


def centred(key, extent, scale, bound, cuts=(), kind=jnp.bfloat16):
    loudness = level_of(key, extent, cuts, -0.22, 0.18) if cuts else 1.0
    values = jax.random.normal(key, extent, jnp.float32) * scale * loudness
    return jnp.minimum(jnp.maximum(values, -bound), bound).astype(kind)


def setup_inputs(seed: int = 0) -> dict:
    streams_of = jax.random.split(jax.random.key(seed), 8)
    loads = draw_loads(jax.random.fold_in(streams_of[7], 71), 0)
    coords = centred(streams_of[1], (DIM, RUNS), 1.0, 6.0, ((1, 64),), jnp.float32)
    coreg_factor = centred(streams_of[2], (CH, CH), CH ** -0.5, 0.375, ((0, 4),), jnp.float32)
    noise = jnp.clip(jnp.exp(math.log(1.0) - 2.3025851 * jax.random.uniform(streams_of[3], (CH,), jnp.float32) ** level_of(streams_of[3], (CH,), ((0, 4),), -0.2, 0.2)), 0.1, 1.0)
    run_perm = draw_run_perm(jax.random.fold_in(streams_of[7], 71), 0)
    block_nbrs = draw_block_nbrs(jax.random.fold_in(streams_of[7], 71), 0)
    nbr_count = draw_nbr_count(jax.random.fold_in(streams_of[7], 71), 0)
    return {"loads": loads, "coords": coords, "coreg_factor": coreg_factor, "noise": noise, "run_perm": run_perm, "block_nbrs": block_nbrs, "nbr_count": nbr_count}


SUPPORT = 5.0
AMPLITUDE = 0.05

def wendland(squared):
    radius_frac = jnp.sqrt(squared) / SUPPORT
    remain = jnp.maximum(1.0 - radius_frac, 0.0)
    cubed = remain * remain * remain
    return cubed * cubed * (6.0 * radius_frac + 1.0)

def apply_operator(operand, coreg, coord_blocks, block_nbrs, nbr_count, noise):
    rounded = operand.astype(jnp.bfloat16)
    mixed = jnp.dot(coreg, rounded.astype(jnp.float32), precision=lax.Precision.HIGHEST)
    mixed_b = mixed.astype(jnp.bfloat16)
    value_blocks = mixed_b.reshape(CH, NBLK, BS)
    own_coords = coord_blocks

    def slot_step(slot_index, summed):
        partner_ids = lax.dynamic_index_in_dim(block_nbrs, slot_index, 1, keepdims=False)
        live_mask = (slot_index < nbr_count).astype(jnp.float32)
        partner = jnp.take(coord_blocks, partner_ids, axis=1)
        squared = jnp.zeros((NBLK, BS, BS), jnp.float32)
        for component in range(DIM):
            difference = own_coords[component][:, :, None] - partner[component][:, None, :]
            squared = squared + difference * difference
        kernel_tile = (wendland(squared) * live_mask[:, None, None]).astype(jnp.bfloat16)
        partner_vals = jnp.take(value_blocks, partner_ids, axis=1)
        return summed + jnp.einsum('bim,cbm->cbi', kernel_tile.astype(jnp.float32), partner_vals.astype(jnp.float32))
    summed = lax.fori_loop(0, MAXC, slot_step, jnp.zeros((CH, NBLK, BS), jnp.float32))
    return AMPLITUDE * summed.reshape(CH, RUNS) + noise[:, None] * operand

def reference(loads, coords, coreg_factor, noise, run_perm, block_nbrs, nbr_count):
    coreg = jnp.dot(coreg_factor, coreg_factor.T, precision=lax.Precision.HIGHEST)
    sorted_coords = jnp.take(coords, run_perm, axis=1)
    sorted_loads = jnp.take(loads, run_perm, axis=1)
    coord_blocks = sorted_coords.reshape(DIM, NBLK, BS)
    iterate = jnp.zeros_like(sorted_loads)
    remainder = sorted_loads
    direction = sorted_loads
    norm_now = jnp.sum(remainder * remainder)
    for iteration in range(ITERS):
        mapped = apply_operator(direction, coreg, coord_blocks, block_nbrs, nbr_count, noise)
        step_size = norm_now / jnp.sum(direction * mapped)
        iterate = iterate + step_size * direction
        remainder = remainder - step_size * mapped
        if iteration + 1 < ITERS:
            norm_next = jnp.sum(remainder * remainder)
            direction = remainder + norm_next / norm_now * direction
            norm_now = norm_next
    solution = jnp.zeros((CH, RUNS), jnp.float32).at[:, run_perm].set(iterate)
    residual = jnp.zeros((CH, RUNS), jnp.float32).at[:, run_perm].set(remainder)
    return (solution, residual)
```

```python
import jax
import jax.numpy as jnp
from jax import lax
from jax.sharding import PartitionSpec as P

ITERS = 2


SUPPORT = 5.0
AMPLITUDE = 0.05


def extended(block, axis, dim, width):
    count = lax.axis_size(axis)
    forward = [(i, i + 1) for i in range(count - 1)]
    backward = [(target, source) for source, target in forward]
    low = lax.ppermute(
        lax.slice_in_dim(block, block.shape[dim] - width, None, axis=dim), axis, forward
    )
    high = lax.ppermute(lax.slice_in_dim(block, 0, width, axis=dim), axis, backward)
    return jnp.concatenate([low, block, high], axis=dim)


def wendland(squared):
    radius_frac = jnp.sqrt(squared) / SUPPORT
    remain = jnp.maximum(1.0 - radius_frac, 0.0)
    cubed = remain * remain * remain
    return cubed * cubed * (6.0 * radius_frac + 1.0)


def global_sum(value):
    for axis in ("chan", "samp"):
        count = lax.axis_size(axis)
        step = 1
        while step < count:
            pairs = [(i, i ^ step) for i in range(count)]
            value = value + lax.ppermute(value, axis, pairs)
            step *= 2
    return value


def per_device(loads, coords, coreg_factor, noise, run_perm, block_nbrs, nbr_count):
    chan_local, runs_local = loads.shape
    blocks_local = nbr_count.shape[0]
    block_runs = runs_local // blocks_local
    dims = coords.shape[0]
    slot_limit = block_nbrs.shape[1]
    halo = slot_limit - 1
    device_pos = lax.axis_index("samp")
    local_perm = run_perm - device_pos * runs_local
    sorted_coords = jnp.take(coords, local_perm, axis=1)
    sorted_loads = jnp.take(loads, local_perm, axis=1)
    norm_now = global_sum(jnp.sum(sorted_loads * sorted_loads))
    full_factor = lax.all_gather(coreg_factor, "chan", axis=0, tiled=True)
    coreg_rows = jnp.dot(coreg_factor, full_factor.T, precision=lax.Precision.HIGHEST)
    reach_runs = halo * block_runs
    window_blocks = blocks_local + 2 * halo
    widened_coords = extended(sorted_coords, "samp", 1, reach_runs)
    coord_blocks = widened_coords.reshape(dims, window_blocks, block_runs)
    own_coords = sorted_coords.reshape(dims, blocks_local, block_runs)
    nbr_local = block_nbrs - (device_pos * blocks_local - halo)
    slot_total = jnp.max(nbr_count)

    def build_tile(slot_index):
        partner_ids = lax.dynamic_index_in_dim(nbr_local, slot_index, 1, keepdims=False)
        live_mask = (slot_index < nbr_count).astype(jnp.float32)
        partner = jnp.take(coord_blocks, partner_ids, axis=1)
        squared = jnp.zeros((blocks_local, block_runs, block_runs), jnp.float32)
        for component in range(dims):
            difference = own_coords[component][:, :, None] - partner[component][:, None, :]
            squared = squared + difference * difference
        return (wendland(squared) * live_mask[:, None, None]).astype(jnp.bfloat16)

    all_tiles = lax.map(build_tile, jnp.arange(slot_limit, dtype=jnp.int32))
    iterate = jnp.zeros_like(sorted_loads)
    remainder = sorted_loads
    direction = sorted_loads
    for iteration in range(ITERS):
        rounded = direction.astype(jnp.bfloat16)
        gathered = lax.all_gather(rounded, "chan", axis=0, tiled=True)
        mixed = jnp.dot(
            coreg_rows, gathered.astype(jnp.float32), precision=lax.Precision.HIGHEST
        )
        mixed_b = mixed.astype(jnp.bfloat16)
        widened = extended(mixed_b, "samp", 1, reach_runs)
        value_blocks = widened.reshape(chan_local, window_blocks, block_runs)

        def slot_step(slot_index, summed):
            partner_ids = lax.dynamic_index_in_dim(nbr_local, slot_index, 1, keepdims=False)
            kernel_tile = lax.dynamic_index_in_dim(all_tiles, slot_index, 0, keepdims=False)
            partner_vals = jnp.take(value_blocks, partner_ids, axis=1)
            return summed + jnp.einsum(
                "bim,cbm->cbi", kernel_tile, partner_vals, preferred_element_type=jnp.float32
            )

        summed = lax.fori_loop(
            0, slot_total, slot_step, jnp.zeros((chan_local, blocks_local, block_runs), jnp.float32)
        )
        mapped = AMPLITUDE * summed.reshape(chan_local, runs_local) + noise[:, None] * direction
        step_size = norm_now / global_sum(jnp.sum(direction * mapped))
        iterate = iterate + step_size * direction
        remainder = remainder - step_size * mapped
        if iteration + 1 < ITERS:
            norm_next = global_sum(jnp.sum(remainder * remainder))
            direction = remainder + norm_next / norm_now * direction
            norm_now = norm_next
    solution = jnp.zeros_like(iterate).at[:, local_perm].set(iterate)
    residual = jnp.zeros_like(remainder).at[:, local_perm].set(remainder)
    return (solution, residual)


def solution(mesh):
    return jax.shard_map(
        per_device,
        mesh=mesh,
        in_specs=(
            P("chan", "samp"),
            P(None, "samp"),
            P("chan", None),
            P("chan"),
            P("samp"),
            P("samp", None),
            P("samp"),
        ),
        out_specs=(P("chan", "samp"), P("chan", "samp")),
        check_vma=False,
    )
```

```python
import functools

import jax
import jax.numpy as jnp
from jax import lax
from jax.experimental import pallas as pl
from jax.experimental.pallas import tpu as pltpu
from jax.sharding import PartitionSpec as P

ITERS = 2
SUPPORT = 5.0
AMPLITUDE = 0.05


def tile_kernel(begin_ref, count_ref, own_ref, win_ref, out_ref, *, slots, dims, runs):
    b = pl.program_id(0)
    start = begin_ref[b]
    count = count_ref[b]
    own = own_ref[0]
    for s in range(slots):
        @pl.when(s < count)
        def _():
            part = win_ref[start + s]
            squared = jnp.zeros((runs, runs), jnp.float32)
            for d in range(dims):
                diff = own[:, d:d + 1] - part[d:d + 1, :]
                squared = squared + diff * diff
            radius_frac = jnp.sqrt(squared) / SUPPORT
            remain = jnp.maximum(1.0 - radius_frac, 0.0)
            cubed = remain * remain * remain
            val = cubed * cubed * (6.0 * radius_frac + 1.0)
            out_ref[0, :, s * runs:(s + 1) * runs] = val.astype(out_ref.dtype)

        @pl.when(s >= count)
        def _():
            out_ref[0, :, s * runs:(s + 1) * runs] = jnp.zeros((runs, runs), out_ref.dtype)


def build_tiles(begin, count, own_t, win_c, slots):
    blocks, runs, dpad = own_t.shape
    kern = functools.partial(tile_kernel, slots=slots, dims=dpad, runs=runs)
    return pl.pallas_call(
        kern,
        grid_spec=pltpu.PrefetchScalarGridSpec(
            num_scalar_prefetch=2,
            grid=(blocks,),
            in_specs=[
                pl.BlockSpec((1, runs, dpad), lambda b, *_: (b, 0, 0)),
                pl.BlockSpec(win_c.shape, lambda b, *_: (0, 0, 0)),
            ],
            out_specs=pl.BlockSpec((1, runs, slots * runs), lambda b, *_: (b, 0, 0)),
        ),
        out_shape=jax.ShapeDtypeStruct((blocks, runs, slots * runs), jnp.bfloat16),
    )(begin, count, own_t, win_c)


def apply_kernel(begin_ref, win_ref, tile_ref, p_ref, noise_ref, out_ref, *, per_step, slots, runs):
    g = pl.program_id(0)
    noise = noise_ref[...]
    for k in range(per_step):
        start = begin_ref[g * per_step + k]
        vals = win_ref[pl.ds(start, slots)]
        cat = jnp.concatenate([vals[s] for s in range(slots)], axis=1)
        acc = lax.dot_general(
            cat, tile_ref[k], (((1,), (1,)), ((), ())), preferred_element_type=jnp.float32
        )
        cols = slice(k * runs, (k + 1) * runs)
        out_ref[:, cols] = AMPLITUDE * acc + noise * p_ref[:, cols]


def apply_operator(begin, win_v, tiles, direction, noise_col, per_step):
    blocks, runs, width = tiles.shape
    slots = width // runs
    chans, total = direction.shape
    kern = functools.partial(apply_kernel, per_step=per_step, slots=slots, runs=runs)
    return pl.pallas_call(
        kern,
        grid_spec=pltpu.PrefetchScalarGridSpec(
            num_scalar_prefetch=1,
            grid=(blocks // per_step,),
            in_specs=[
                pl.BlockSpec(win_v.shape, lambda g, *_: (0, 0, 0)),
                pl.BlockSpec((per_step, runs, width), lambda g, *_: (g, 0, 0)),
                pl.BlockSpec((chans, per_step * runs), lambda g, *_: (0, g)),
                pl.BlockSpec((chans, 1), lambda g, *_: (0, 0)),
            ],
            out_specs=pl.BlockSpec((chans, per_step * runs), lambda g, *_: (0, g)),
        ),
        out_shape=jax.ShapeDtypeStruct((chans, total), jnp.float32),
    )(begin, win_v, tiles, direction, noise_col)


def extended(block, axis, dim, width):
    count = lax.axis_size(axis)
    forward = [(i, i + 1) for i in range(count - 1)]
    backward = [(target, source) for source, target in forward]
    low = lax.ppermute(
        lax.slice_in_dim(block, block.shape[dim] - width, None, axis=dim), axis, forward
    )
    high = lax.ppermute(lax.slice_in_dim(block, 0, width, axis=dim), axis, backward)
    return jnp.concatenate([low, block, high], axis=dim)


def global_sum(value):
    for axis in ("chan", "samp"):
        count = lax.axis_size(axis)
        step = 1
        while step < count:
            pairs = [(i, i ^ step) for i in range(count)]
            value = value + lax.ppermute(value, axis, pairs)
            step *= 2
    return value


def gather_chan(rounded):
    count = lax.axis_size("chan")
    parts = [rounded]
    for shift in range(1, count):
        pairs = [((i + shift) % count, i) for i in range(count)]
        parts.append(lax.ppermute(rounded, "chan", pairs))
    return jnp.concatenate(parts, axis=0)


def per_device(loads, coords, coreg_factor, noise, run_perm, block_nbrs, nbr_count):
    chan_local, runs_local = loads.shape
    blocks_local = nbr_count.shape[0]
    block_runs = runs_local // blocks_local
    dims = coords.shape[0]
    dpad = 8
    slot_limit = block_nbrs.shape[1]
    halo = slot_limit - 1
    device_pos = lax.axis_index("samp")
    chan_pos = lax.axis_index("chan")
    local_perm = run_perm - device_pos * runs_local
    sorted_coords = jnp.take(coords, local_perm, axis=1)
    sorted_loads = jnp.take(loads, local_perm, axis=1)
    norm_now = global_sum(jnp.sum(sorted_loads * sorted_loads))
    full_factor = lax.all_gather(coreg_factor, "chan", axis=0, tiled=True)
    coreg_rows = jnp.dot(coreg_factor, full_factor.T, precision=lax.Precision.HIGHEST)
    coreg_perm = jnp.roll(coreg_rows, -chan_pos * chan_local, axis=1)
    reach_runs = halo * block_runs
    window_blocks = blocks_local + 2 * halo
    widened_coords = extended(sorted_coords, "samp", 1, reach_runs)
    win_c = jnp.pad(
        widened_coords.reshape(dims, window_blocks, block_runs), ((0, dpad - dims), (0, 0), (0, 0))
    ).transpose(1, 0, 2)
    own_t = jnp.pad(
        sorted_coords.reshape(dims, blocks_local, block_runs), ((0, dpad - dims), (0, 0), (0, 0))
    ).transpose(1, 2, 0)
    begin = jnp.clip(
        block_nbrs[:, 0] - (device_pos * blocks_local - halo), 0, window_blocks - slot_limit
    ).astype(jnp.int32)
    tiles = build_tiles(begin, nbr_count.astype(jnp.int32), own_t, win_c, slot_limit)
    noise_col = noise[:, None]
    iterate = jnp.zeros_like(sorted_loads)
    remainder = sorted_loads
    direction = sorted_loads
    for iteration in range(ITERS):
        rounded = direction.astype(jnp.bfloat16)
        gathered = gather_chan(rounded)
        mixed = jnp.dot(
            coreg_perm, gathered.astype(jnp.float32), precision=lax.Precision.HIGHEST
        )
        mixed_b = mixed.astype(jnp.bfloat16)
        widened = extended(mixed_b, "samp", 1, reach_runs)
        win_v = widened.reshape(chan_local, window_blocks, block_runs).transpose(1, 0, 2)
        mapped = apply_operator(begin, win_v, tiles, direction, noise_col, 4)
        step_size = norm_now / global_sum(jnp.sum(direction * mapped))
        iterate = iterate + step_size * direction
        remainder = remainder - step_size * mapped
        if iteration + 1 < ITERS:
            norm_next = global_sum(jnp.sum(remainder * remainder))
            direction = remainder + norm_next / norm_now * direction
            norm_now = norm_next
    solution = jnp.zeros_like(iterate).at[:, local_perm].set(iterate)
    residual = jnp.zeros_like(remainder).at[:, local_perm].set(remainder)
    return (solution, residual)


def solution(mesh):
    return jax.shard_map(
        per_device,
        mesh=mesh,
        in_specs=(
            P("chan", "samp"),
            P(None, "samp"),
            P("chan", None),
            P("chan"),
            P("samp"),
            P("samp", None),
            P("samp"),
        ),
        out_specs=(P("chan", "samp"), P("chan", "samp")),
        check_vma=False,
    )
```

```python
import functools

import jax
import jax.numpy as jnp
from jax import lax
from jax.experimental import pallas as pl
from jax.experimental.pallas import tpu as pltpu
from jax.sharding import PartitionSpec as P

ITERS = 2
SUPPORT = 5.0
AMPLITUDE = 0.05


def tile_kernel(begin_ref, count_ref, own_ref, win_ref, out_ref, *, slots, runs):
    b = pl.program_id(0)
    start = begin_ref[b]
    count = count_ref[b]
    own = own_ref[0]
    parts = jnp.concatenate([win_ref[start + s] for s in range(slots)], axis=1)
    cross = jnp.dot(
        own * -2.0, parts, precision=lax.Precision.HIGHEST, preferred_element_type=jnp.float32
    )
    own_sq = jnp.sum(own * own, axis=1, keepdims=True)
    part_sq = jnp.sum(parts * parts, axis=0, keepdims=True)
    for s in range(slots):
        cols = slice(s * runs, (s + 1) * runs)

        @pl.when(s < count)
        def _():
            squared = jnp.maximum((own_sq + part_sq[:, cols]) + cross[:, cols], 0.0)
            radius_frac = jnp.sqrt(squared) * (1.0 / SUPPORT)
            remain = jnp.maximum(1.0 - radius_frac, 0.0)
            cubed = remain * remain * remain
            val = cubed * cubed * (6.0 * radius_frac + 1.0)
            out_ref[0, :, cols] = val.astype(out_ref.dtype)

        @pl.when(s >= count)
        def _():
            out_ref[0, :, cols] = jnp.zeros((runs, runs), out_ref.dtype)


def build_tiles(begin, count, own_t, win_c, slots):
    blocks, runs, dpad = own_t.shape
    kern = functools.partial(tile_kernel, slots=slots, runs=runs)
    return pl.pallas_call(
        kern,
        grid_spec=pltpu.PrefetchScalarGridSpec(
            num_scalar_prefetch=2,
            grid=(blocks,),
            in_specs=[
                pl.BlockSpec((1, runs, dpad), lambda b, *_: (b, 0, 0)),
                pl.BlockSpec(win_c.shape, lambda b, *_: (0, 0, 0)),
            ],
            out_specs=pl.BlockSpec((1, runs, slots * runs), lambda b, *_: (b, 0, 0)),
        ),
        out_shape=jax.ShapeDtypeStruct((blocks, runs, slots * runs), jnp.bfloat16),
    )(begin, count, own_t, win_c)


def apply_kernel(begin_ref, win_ref, tile_ref, p_ref, noise_ref, out_ref, *, per_step, slots, runs):
    g = pl.program_id(0)
    noise = noise_ref[...]
    for k in range(per_step):
        start = begin_ref[g * per_step + k]
        vals = win_ref[pl.ds(start, slots)]
        cat = jnp.concatenate([vals[s] for s in range(slots)], axis=1)
        acc = lax.dot_general(
            cat, tile_ref[k], (((1,), (1,)), ((), ())), preferred_element_type=jnp.float32
        )
        cols = slice(k * runs, (k + 1) * runs)
        out_ref[:, cols] = AMPLITUDE * acc + noise * p_ref[:, cols]


def apply_operator(begin, win_v, tiles, direction, noise_col, per_step):
    blocks, runs, width = tiles.shape
    slots = width // runs
    chans, total = direction.shape
    kern = functools.partial(apply_kernel, per_step=per_step, slots=slots, runs=runs)
    return pl.pallas_call(
        kern,
        grid_spec=pltpu.PrefetchScalarGridSpec(
            num_scalar_prefetch=1,
            grid=(blocks // per_step,),
            in_specs=[
                pl.BlockSpec(win_v.shape, lambda g, *_: (0, 0, 0)),
                pl.BlockSpec((per_step, runs, width), lambda g, *_: (g, 0, 0)),
                pl.BlockSpec((chans, per_step * runs), lambda g, *_: (0, g)),
                pl.BlockSpec((chans, 1), lambda g, *_: (0, 0)),
            ],
            out_specs=pl.BlockSpec((chans, per_step * runs), lambda g, *_: (0, g)),
        ),
        out_shape=jax.ShapeDtypeStruct((chans, total), jnp.float32),
    )(begin, win_v, tiles, direction, noise_col)


def extended(block, axis, dim, width):
    count = lax.axis_size(axis)
    forward = [(i, i + 1) for i in range(count - 1)]
    backward = [(target, source) for source, target in forward]
    low = lax.ppermute(
        lax.slice_in_dim(block, block.shape[dim] - width, None, axis=dim), axis, forward
    )
    high = lax.ppermute(lax.slice_in_dim(block, 0, width, axis=dim), axis, backward)
    return jnp.concatenate([low, block, high], axis=dim)


def global_sum(value):
    for axis in ("chan", "samp"):
        count = lax.axis_size(axis)
        step = 1
        while step < count:
            pairs = [(i, i ^ step) for i in range(count)]
            value = value + lax.ppermute(value, axis, pairs)
            step *= 2
    return value


def gather_chan(rounded):
    count = lax.axis_size("chan")
    parts = [rounded]
    for shift in range(1, count):
        pairs = [((i + shift) % count, i) for i in range(count)]
        parts.append(lax.ppermute(rounded, "chan", pairs))
    return jnp.concatenate(parts, axis=0)


def per_device(loads, coords, coreg_factor, noise, run_perm, block_nbrs, nbr_count):
    chan_local, runs_local = loads.shape
    blocks_local = nbr_count.shape[0]
    block_runs = runs_local // blocks_local
    dims = coords.shape[0]
    dpad = 8
    slot_limit = block_nbrs.shape[1]
    halo = slot_limit - 1
    device_pos = lax.axis_index("samp")
    local_perm = run_perm - device_pos * runs_local
    sorted_coords = jnp.take(coords, local_perm, axis=1)
    sorted_loads = jnp.take(loads, local_perm, axis=1)
    norm_local = jnp.sum(sorted_loads * sorted_loads)
    coreg_perm = jnp.dot(
        coreg_factor, gather_chan(coreg_factor).T, precision=lax.Precision.HIGHEST
    )
    reach_runs = halo * block_runs
    window_blocks = blocks_local + 2 * halo
    widened_coords = extended(sorted_coords, "samp", 1, reach_runs)
    win_c = jnp.pad(
        widened_coords.reshape(dims, window_blocks, block_runs), ((0, dpad - dims), (0, 0), (0, 0))
    ).transpose(1, 0, 2)
    own_t = jnp.pad(
        sorted_coords.reshape(dims, blocks_local, block_runs), ((0, dpad - dims), (0, 0), (0, 0))
    ).transpose(1, 2, 0)
    begin = jnp.clip(
        block_nbrs[:, 0] - (device_pos * blocks_local - halo), 0, window_blocks - slot_limit
    ).astype(jnp.int32)
    tiles = build_tiles(begin, nbr_count.astype(jnp.int32), own_t, win_c, slot_limit)
    noise_col = noise[:, None]
    iterate = jnp.zeros_like(sorted_loads)
    remainder = sorted_loads
    direction = sorted_loads
    for iteration in range(ITERS):
        rounded = direction.astype(jnp.bfloat16)
        gathered = gather_chan(rounded)
        mixed = jnp.dot(
            coreg_perm, gathered.astype(jnp.float32), precision=lax.Precision.HIGHEST
        )
        mixed_b = mixed.astype(jnp.bfloat16)
        widened = extended(mixed_b, "samp", 1, reach_runs)
        win_v = widened.reshape(chan_local, window_blocks, block_runs).transpose(1, 0, 2)
        mapped = apply_operator(begin, win_v, tiles, direction, noise_col, 4)
        curvature = jnp.sum(direction * mapped)
        if iteration == 0:
            sums = global_sum(jnp.stack([norm_local, curvature]))
            norm_now, curvature = sums[0], sums[1]
        else:
            curvature = global_sum(curvature)
        step_size = norm_now / curvature
        iterate = iterate + step_size * direction
        remainder = remainder - step_size * mapped
        if iteration + 1 < ITERS:
            norm_next = global_sum(jnp.sum(remainder * remainder))
            direction = remainder + norm_next / norm_now * direction
            norm_now = norm_next
    solution = jnp.zeros_like(iterate).at[:, local_perm].set(iterate)
    residual = jnp.zeros_like(remainder).at[:, local_perm].set(remainder)
    return (solution, residual)


def solution(mesh):
    return jax.shard_map(
        per_device,
        mesh=mesh,
        in_specs=(
            P("chan", "samp"),
            P(None, "samp"),
            P("chan", None),
            P("chan"),
            P("samp"),
            P("samp", None),
            P("samp"),
        ),
        out_specs=(P("chan", "samp"), P("chan", "samp")),
        check_vma=False,
    )
```

```python
import functools

import jax
import jax.numpy as jnp
from jax import lax
from jax.experimental import pallas as pl
from jax.experimental.pallas import tpu as pltpu
from jax.sharding import PartitionSpec as P

ITERS = 2
SUPPORT = 5.0
AMPLITUDE = 0.05


def tile_kernel(begin_ref, count_ref, own_ref, win_ref, out_ref, *, slots, runs):
    b = pl.program_id(0)
    start = begin_ref[b]
    count = count_ref[b]
    own = own_ref[0]
    parts = jnp.concatenate([win_ref[start + s] for s in range(slots)], axis=1)
    cross = jnp.dot(
        own * -2.0, parts, precision=lax.Precision.HIGHEST, preferred_element_type=jnp.float32
    )
    own_sq = jnp.sum(own * own, axis=1, keepdims=True)
    part_sq = jnp.sum(parts * parts, axis=0, keepdims=True)
    for s in range(slots):
        cols = slice(s * runs, (s + 1) * runs)

        @pl.when(s < count)
        def _():
            squared = jnp.maximum((own_sq + part_sq[:, cols]) + cross[:, cols], 0.0)
            radius_frac = jnp.sqrt(squared) * (1.0 / SUPPORT)
            remain = jnp.maximum(1.0 - radius_frac, 0.0)
            cubed = remain * remain * remain
            val = cubed * cubed * (6.0 * radius_frac + 1.0)
            out_ref[0, :, cols] = val.astype(out_ref.dtype)

        @pl.when(s >= count)
        def _():
            out_ref[0, :, cols] = jnp.zeros((runs, runs), out_ref.dtype)


def build_tiles(begin, count, own_t, win_c, slots):
    blocks, runs, dpad = own_t.shape
    kern = functools.partial(tile_kernel, slots=slots, runs=runs)
    return pl.pallas_call(
        kern,
        grid_spec=pltpu.PrefetchScalarGridSpec(
            num_scalar_prefetch=2,
            grid=(blocks,),
            in_specs=[
                pl.BlockSpec((1, runs, dpad), lambda b, *_: (b, 0, 0)),
                pl.BlockSpec(win_c.shape, lambda b, *_: (0, 0, 0)),
            ],
            out_specs=pl.BlockSpec((1, runs, slots * runs), lambda b, *_: (b, 0, 0)),
        ),
        out_shape=jax.ShapeDtypeStruct((blocks, runs, slots * runs), jnp.bfloat16),
    )(begin, count, own_t, win_c)


def apply_kernel(begin_ref, win_ref, tile_ref, p_ref, noise_ref, out_ref, *, per_step, slots, runs):
    g = pl.program_id(0)
    noise = noise_ref[...]
    for k in range(per_step):
        start = begin_ref[g * per_step + k]
        vals = win_ref[pl.ds(start, slots)]
        cat = jnp.concatenate([vals[s] for s in range(slots)], axis=1)
        acc = lax.dot_general(
            cat, tile_ref[k], (((1,), (1,)), ((), ())), preferred_element_type=jnp.float32
        )
        cols = slice(k * runs, (k + 1) * runs)
        out_ref[:, cols] = AMPLITUDE * acc + noise * p_ref[:, cols]


def apply_operator(begin, win_v, tiles, direction, noise_col, per_step):
    blocks, runs, width = tiles.shape
    slots = width // runs
    chans, total = direction.shape
    kern = functools.partial(apply_kernel, per_step=per_step, slots=slots, runs=runs)
    return pl.pallas_call(
        kern,
        grid_spec=pltpu.PrefetchScalarGridSpec(
            num_scalar_prefetch=1,
            grid=(blocks // per_step,),
            in_specs=[
                pl.BlockSpec(win_v.shape, lambda g, *_: (0, 0, 0)),
                pl.BlockSpec((per_step, runs, width), lambda g, *_: (g, 0, 0)),
                pl.BlockSpec((chans, per_step * runs), lambda g, *_: (0, g)),
                pl.BlockSpec((chans, 1), lambda g, *_: (0, 0)),
            ],
            out_specs=pl.BlockSpec((chans, per_step * runs), lambda g, *_: (0, g)),
        ),
        out_shape=jax.ShapeDtypeStruct((chans, total), jnp.float32),
    )(begin, win_v, tiles, direction, noise_col)


def extended(block, axis, dim, width):
    count = lax.axis_size(axis)
    forward = [(i, i + 1) for i in range(count - 1)]
    backward = [(target, source) for source, target in forward]
    low = lax.ppermute(
        lax.slice_in_dim(block, block.shape[dim] - width, None, axis=dim), axis, forward
    )
    high = lax.ppermute(lax.slice_in_dim(block, 0, width, axis=dim), axis, backward)
    return jnp.concatenate([low, block, high], axis=dim)


def global_sum(value):
    for axis in ("chan", "samp"):
        count = lax.axis_size(axis)
        step = 1
        while step < count:
            pairs = [(i, i ^ step) for i in range(count)]
            value = value + lax.ppermute(value, axis, pairs)
            step *= 2
    return value


def gather_chan(rounded):
    count = lax.axis_size("chan")
    parts = [rounded]
    for shift in range(1, count):
        pairs = [((i + shift) % count, i) for i in range(count)]
        parts.append(lax.ppermute(rounded, "chan", pairs))
    return jnp.concatenate(parts, axis=0)


def per_device(loads, coords, coreg_factor, noise, run_perm, block_nbrs, nbr_count):
    chan_local, runs_local = loads.shape
    blocks_local = nbr_count.shape[0]
    block_runs = runs_local // blocks_local
    dims = coords.shape[0]
    dpad = 8
    slot_limit = block_nbrs.shape[1]
    halo = slot_limit - 1
    device_pos = lax.axis_index("samp")
    local_perm = run_perm - device_pos * runs_local
    sorted_both = jnp.take(jnp.concatenate([coords, loads], axis=0), local_perm, axis=1)
    sorted_coords = sorted_both[:dims]
    sorted_loads = sorted_both[dims:]
    norm_local = jnp.sum(sorted_loads * sorted_loads)
    coreg_perm = jnp.dot(
        coreg_factor, gather_chan(coreg_factor).T, precision=lax.Precision.HIGHEST
    )
    reach_runs = halo * block_runs
    window_blocks = blocks_local + 2 * halo
    widened_coords = extended(sorted_coords, "samp", 1, reach_runs)
    win_c = jnp.pad(
        widened_coords.reshape(dims, window_blocks, block_runs), ((0, dpad - dims), (0, 0), (0, 0))
    ).transpose(1, 0, 2)
    own_t = jnp.pad(
        sorted_coords.reshape(dims, blocks_local, block_runs), ((0, dpad - dims), (0, 0), (0, 0))
    ).transpose(1, 2, 0)
    begin = jnp.clip(
        block_nbrs[:, 0] - (device_pos * blocks_local - halo), 0, window_blocks - slot_limit
    ).astype(jnp.int32)
    tiles = build_tiles(begin, nbr_count.astype(jnp.int32), own_t, win_c, slot_limit)
    noise_col = noise[:, None]
    iterate = jnp.zeros_like(sorted_loads)
    remainder = sorted_loads
    direction = sorted_loads
    for iteration in range(ITERS):
        rounded = direction.astype(jnp.bfloat16)
        gathered = gather_chan(rounded)
        mixed = jnp.dot(
            coreg_perm, gathered.astype(jnp.float32), precision=lax.Precision.HIGHEST
        )
        mixed_b = mixed.astype(jnp.bfloat16)
        widened = extended(mixed_b, "samp", 1, reach_runs)
        win_v = widened.reshape(chan_local, window_blocks, block_runs).transpose(1, 0, 2)
        mapped = apply_operator(begin, win_v, tiles, direction, noise_col, 4)
        curvature = jnp.sum(direction * mapped)
        if iteration + 1 == ITERS:
            stacked = jnp.concatenate([iterate, remainder, direction, mapped], axis=0)
            unsorted = jnp.zeros_like(stacked).at[:, local_perm].set(stacked)
            iterate, remainder, direction, mapped = jnp.split(unsorted, 4, axis=0)
        if iteration == 0:
            sums = global_sum(jnp.stack([norm_local, curvature]))
            norm_now, curvature = sums[0], sums[1]
        else:
            curvature = global_sum(curvature)
        step_size = norm_now / curvature
        iterate = iterate + step_size * direction
        remainder = remainder - step_size * mapped
        if iteration + 1 < ITERS:
            norm_next = global_sum(jnp.sum(remainder * remainder))
            direction = remainder + norm_next / norm_now * direction
            norm_now = norm_next
    return (iterate, remainder)


def solution(mesh):
    return jax.shard_map(
        per_device,
        mesh=mesh,
        in_specs=(
            P("chan", "samp"),
            P(None, "samp"),
            P("chan", None),
            P("chan"),
            P("samp"),
            P("samp", None),
            P("samp"),
        ),
        out_specs=(P("chan", "samp"), P("chan", "samp")),
        check_vma=False,
    )
```

```python
import functools

import jax
import jax.numpy as jnp
from jax import lax
from jax.experimental import pallas as pl
from jax.experimental.pallas import tpu as pltpu
from jax.sharding import PartitionSpec as P

ITERS = 2
SUPPORT = 5.0
AMPLITUDE = 0.05


def tile_kernel(begin_ref, count_ref, own_ref, win_ref, out_ref, *, slots, runs):
    b = pl.program_id(0)
    start = begin_ref[b]
    count = count_ref[b]
    own = own_ref[0]
    parts = jnp.concatenate([win_ref[start + s] for s in range(slots)], axis=1)
    cross = jnp.dot(own, parts, precision=lax.Precision.HIGHEST, preferred_element_type=jnp.float32)
    for s in range(slots):
        cols = slice(s * runs, (s + 1) * runs)

        @pl.when(s < count)
        def _():
            squared = jnp.maximum(cross[:, cols], 0.0)
            radius_frac = jnp.sqrt(squared) * (1.0 / SUPPORT)
            remain = jnp.maximum(1.0 - radius_frac, 0.0)
            cubed = remain * remain * remain
            val = cubed * cubed * (6.0 * radius_frac + 1.0)
            out_ref[0, :, cols] = val.astype(out_ref.dtype)

        @pl.when(s >= count)
        def _():
            out_ref[0, :, cols] = jnp.zeros((runs, runs), out_ref.dtype)


def build_tiles(begin, count, own_t, win_c, slots):
    blocks, runs, dpad = own_t.shape
    kern = functools.partial(tile_kernel, slots=slots, runs=runs)
    return pl.pallas_call(
        kern,
        grid_spec=pltpu.PrefetchScalarGridSpec(
            num_scalar_prefetch=2,
            grid=(blocks,),
            in_specs=[
                pl.BlockSpec((1, runs, dpad), lambda b, *_: (b, 0, 0)),
                pl.BlockSpec(win_c.shape, lambda b, *_: (0, 0, 0)),
            ],
            out_specs=pl.BlockSpec((1, runs, slots * runs), lambda b, *_: (b, 0, 0)),
        ),
        out_shape=jax.ShapeDtypeStruct((blocks, runs, slots * runs), jnp.bfloat16),
    )(begin, count, own_t, win_c)


def apply_kernel(begin_ref, win_ref, tile_ref, p_ref, noise_ref, out_ref, *, per_step, slots, runs):
    g = pl.program_id(0)
    noise = noise_ref[...]
    for k in range(per_step):
        start = begin_ref[g * per_step + k]
        vals = win_ref[pl.ds(start, slots)]
        cat = jnp.concatenate([vals[s] for s in range(slots)], axis=1)
        acc = lax.dot_general(
            cat, tile_ref[k], (((1,), (1,)), ((), ())), preferred_element_type=jnp.float32
        )
        cols = slice(k * runs, (k + 1) * runs)
        out_ref[:, cols] = AMPLITUDE * acc + noise * p_ref[:, cols]


def apply_operator(begin, win_v, tiles, direction, noise_col, per_step):
    blocks, runs, width = tiles.shape
    slots = width // runs
    chans, total = direction.shape
    kern = functools.partial(apply_kernel, per_step=per_step, slots=slots, runs=runs)
    return pl.pallas_call(
        kern,
        grid_spec=pltpu.PrefetchScalarGridSpec(
            num_scalar_prefetch=1,
            grid=(blocks // per_step,),
            in_specs=[
                pl.BlockSpec(win_v.shape, lambda g, *_: (0, 0, 0)),
                pl.BlockSpec((per_step, runs, width), lambda g, *_: (g, 0, 0)),
                pl.BlockSpec((chans, per_step * runs), lambda g, *_: (0, g)),
                pl.BlockSpec((chans, 1), lambda g, *_: (0, 0)),
            ],
            out_specs=pl.BlockSpec((chans, per_step * runs), lambda g, *_: (0, g)),
        ),
        out_shape=jax.ShapeDtypeStruct((chans, total), jnp.float32),
    )(begin, win_v, tiles, direction, noise_col)


def extended(block, axis, dim, width):
    count = lax.axis_size(axis)
    forward = [(i, i + 1) for i in range(count - 1)]
    backward = [(target, source) for source, target in forward]
    low = lax.ppermute(
        lax.slice_in_dim(block, block.shape[dim] - width, None, axis=dim), axis, forward
    )
    high = lax.ppermute(lax.slice_in_dim(block, 0, width, axis=dim), axis, backward)
    return jnp.concatenate([low, block, high], axis=dim)


def global_sum(value):
    for axis in ("chan", "samp"):
        count = lax.axis_size(axis)
        step = 1
        while step < count:
            pairs = [(i, i ^ step) for i in range(count)]
            value = value + lax.ppermute(value, axis, pairs)
            step *= 2
    return value


def gather_chan(rounded):
    count = lax.axis_size("chan")
    parts = [rounded]
    for shift in range(1, count):
        pairs = [((i + shift) % count, i) for i in range(count)]
        parts.append(lax.ppermute(rounded, "chan", pairs))
    return jnp.concatenate(parts, axis=0)


def per_device(loads, coords, coreg_factor, noise, run_perm, block_nbrs, nbr_count):
    chan_local, runs_local = loads.shape
    blocks_local = nbr_count.shape[0]
    block_runs = runs_local // blocks_local
    dims = coords.shape[0]
    dpad = 8
    slot_limit = block_nbrs.shape[1]
    halo = slot_limit - 1
    device_pos = lax.axis_index("samp")
    local_perm = run_perm - device_pos * runs_local
    sorted_both = jnp.take(jnp.concatenate([coords, loads], axis=0), local_perm, axis=1)
    sorted_coords = sorted_both[:dims]
    sorted_loads = sorted_both[dims:]
    norm_local = jnp.sum(sorted_loads * sorted_loads)
    coreg_perm = jnp.dot(
        coreg_factor, gather_chan(coreg_factor).T, precision=lax.Precision.HIGHEST
    )
    reach_runs = halo * block_runs
    window_blocks = blocks_local + 2 * halo
    widened_coords = extended(sorted_coords, "samp", 1, reach_runs)
    part_sq = jnp.sum(widened_coords * widened_coords, axis=0, keepdims=True)
    win_c = jnp.concatenate(
        [widened_coords, jnp.ones_like(part_sq), part_sq], axis=0
    ).reshape(dpad, window_blocks, block_runs).transpose(1, 0, 2)
    own_sq = jnp.sum(sorted_coords * sorted_coords, axis=0, keepdims=True)
    own_t = jnp.concatenate(
        [sorted_coords * -2.0, own_sq, jnp.ones_like(own_sq)], axis=0
    ).reshape(dpad, blocks_local, block_runs).transpose(1, 2, 0)
    begin = jnp.clip(
        block_nbrs[:, 0] - (device_pos * blocks_local - halo), 0, window_blocks - slot_limit
    ).astype(jnp.int32)
    counts = nbr_count.astype(jnp.int32)
    half = blocks_local // 2
    tiles_lo = build_tiles(begin[:half], counts[:half], own_t[:half], win_c, slot_limit)
    noise_col = noise[:, None]
    iterate = jnp.zeros_like(sorted_loads)
    remainder = sorted_loads
    direction = sorted_loads
    for iteration in range(ITERS):
        rounded = direction.astype(jnp.bfloat16)
        gathered = gather_chan(rounded)
        if iteration == 0:
            tiles_lo, gathered, coreg_perm = lax.optimization_barrier(
                (tiles_lo, gathered, coreg_perm)
            )
            tiles_hi = build_tiles(begin[half:], counts[half:], own_t[half:], win_c, slot_limit)
            tiles = jnp.concatenate([tiles_lo, tiles_hi], axis=0)
        mixed = jnp.dot(
            coreg_perm, gathered.astype(jnp.float32), precision=lax.Precision.HIGHEST
        )
        mixed_b = mixed.astype(jnp.bfloat16)
        widened = extended(mixed_b, "samp", 1, reach_runs)
        win_v = widened.reshape(chan_local, window_blocks, block_runs).transpose(1, 0, 2)
        mapped = apply_operator(begin, win_v, tiles, direction, noise_col, 4)
        curvature = jnp.sum(direction * mapped)
        if iteration + 1 == ITERS:
            stacked = jnp.concatenate([direction, mapped], axis=0)
            unsorted = jnp.zeros_like(stacked).at[:, local_perm].set(stacked)
            direction, mapped = jnp.split(unsorted, 2, axis=0)
            iterate, remainder = jnp.split(early, 2, axis=0)
        if iteration == 0:
            sums = global_sum(jnp.stack([norm_local, curvature]))
            norm_now, curvature = sums[0], sums[1]
        else:
            curvature = global_sum(curvature)
        step_size = norm_now / curvature
        iterate = iterate + step_size * direction
        remainder = remainder - step_size * mapped
        if iteration + 2 == ITERS:
            both = jnp.concatenate([iterate, remainder], axis=0)
            early = jnp.zeros_like(both).at[:, local_perm].set(both)
        if iteration + 1 < ITERS:
            norm_next = global_sum(jnp.sum(remainder * remainder))
            direction = remainder + norm_next / norm_now * direction
            norm_now = norm_next
    return (iterate, remainder)


def solution(mesh):
    return jax.shard_map(
        per_device,
        mesh=mesh,
        in_specs=(
            P("chan", "samp"),
            P(None, "samp"),
            P("chan", None),
            P("chan"),
            P("samp"),
            P("samp", None),
            P("samp"),
        ),
        out_specs=(P("chan", "samp"), P("chan", "samp")),
        check_vma=False,
    )
```

```python
import functools

import jax
import jax.numpy as jnp
from jax import lax
from jax.experimental import pallas as pl
from jax.experimental.pallas import tpu as pltpu
from jax.sharding import PartitionSpec as P

ITERS = 2
SUPPORT = 5.0
AMPLITUDE = 0.05


def tile_kernel(begin_ref, count_ref, own_ref, win_ref, out_ref, *, slots, runs):
    b = pl.program_id(0)
    start = begin_ref[b]
    count = count_ref[b]
    own = own_ref[0]
    for s in range(slots):
        cols = slice(s * runs, (s + 1) * runs)

        @pl.when(s < count)
        def _():
            cross = jnp.dot(
                own, win_ref[start + s], precision=lax.Precision.HIGHEST,
                preferred_element_type=jnp.float32,
            )
            squared = jnp.maximum(cross, 0.0)
            radius_frac = jnp.sqrt(squared) * (1.0 / SUPPORT)
            remain = jnp.maximum(1.0 - radius_frac, 0.0)
            cubed = remain * remain * remain
            val = cubed * cubed * (6.0 * radius_frac + 1.0)
            out_ref[0, :, cols] = val.astype(out_ref.dtype)

        @pl.when(s >= count)
        def _():
            out_ref[0, :, cols] = jnp.zeros((runs, runs), out_ref.dtype)


def build_tiles(begin, count, own_t, win_c, slots):
    blocks, runs, dpad = own_t.shape
    kern = functools.partial(tile_kernel, slots=slots, runs=runs)
    return pl.pallas_call(
        kern,
        grid_spec=pltpu.PrefetchScalarGridSpec(
            num_scalar_prefetch=2,
            grid=(blocks,),
            in_specs=[
                pl.BlockSpec((1, runs, dpad), lambda b, *_: (b, 0, 0)),
                pl.BlockSpec(win_c.shape, lambda b, *_: (0, 0, 0)),
            ],
            out_specs=pl.BlockSpec((1, runs, slots * runs), lambda b, *_: (b, 0, 0)),
        ),
        out_shape=jax.ShapeDtypeStruct((blocks, runs, slots * runs), jnp.bfloat16),
    )(begin, count, own_t, win_c)


def apply_kernel(begin_ref, win_ref, tile_ref, p_ref, noise_ref, out_ref, *, per_step, slots, runs):
    g = pl.program_id(0)
    noise = noise_ref[...]
    for k in range(per_step):
        start = begin_ref[g * per_step + k]
        vals = win_ref[pl.ds(start, slots)]
        cat = jnp.concatenate([vals[s] for s in range(slots)], axis=1)
        acc = lax.dot_general(
            cat, tile_ref[k], (((1,), (1,)), ((), ())), preferred_element_type=jnp.float32
        )
        cols = slice(k * runs, (k + 1) * runs)
        out_ref[:, cols] = AMPLITUDE * acc + noise * p_ref[:, cols]


def apply_operator(begin, win_v, tiles, direction, noise_col, per_step):
    blocks, runs, width = tiles.shape
    slots = width // runs
    chans, total = direction.shape
    kern = functools.partial(apply_kernel, per_step=per_step, slots=slots, runs=runs)
    return pl.pallas_call(
        kern,
        grid_spec=pltpu.PrefetchScalarGridSpec(
            num_scalar_prefetch=1,
            grid=(blocks // per_step,),
            in_specs=[
                pl.BlockSpec(win_v.shape, lambda g, *_: (0, 0, 0)),
                pl.BlockSpec((per_step, runs, width), lambda g, *_: (g, 0, 0)),
                pl.BlockSpec((chans, per_step * runs), lambda g, *_: (0, g)),
                pl.BlockSpec((chans, 1), lambda g, *_: (0, 0)),
            ],
            out_specs=pl.BlockSpec((chans, per_step * runs), lambda g, *_: (0, g)),
        ),
        out_shape=jax.ShapeDtypeStruct((chans, total), jnp.float32),
    )(begin, win_v, tiles, direction, noise_col)


def extended(block, axis, dim, width):
    count = lax.axis_size(axis)
    forward = [(i, i + 1) for i in range(count - 1)]
    backward = [(target, source) for source, target in forward]
    low = lax.ppermute(
        lax.slice_in_dim(block, block.shape[dim] - width, None, axis=dim), axis, forward
    )
    high = lax.ppermute(lax.slice_in_dim(block, 0, width, axis=dim), axis, backward)
    return jnp.concatenate([low, block, high], axis=dim)


def global_sum(value):
    for axis in ("chan", "samp"):
        count = lax.axis_size(axis)
        step = 1
        while step < count:
            pairs = [(i, i ^ step) for i in range(count)]
            value = value + lax.ppermute(value, axis, pairs)
            step *= 2
    return value


def gather_chan(rounded):
    count = lax.axis_size("chan")
    parts = [rounded]
    for shift in range(1, count):
        pairs = [((i + shift) % count, i) for i in range(count)]
        parts.append(lax.ppermute(rounded, "chan", pairs))
    return jnp.concatenate(parts, axis=0)


def per_device(loads, coords, coreg_factor, noise, run_perm, block_nbrs, nbr_count):
    chan_local, runs_local = loads.shape
    blocks_local = nbr_count.shape[0]
    block_runs = runs_local // blocks_local
    dims = coords.shape[0]
    dpad = 8
    slot_limit = block_nbrs.shape[1]
    halo = slot_limit - 1
    device_pos = lax.axis_index("samp")
    local_perm = run_perm - device_pos * runs_local
    sorted_both = jnp.take(jnp.concatenate([coords, loads], axis=0), local_perm, axis=1)
    sorted_coords = sorted_both[:dims]
    sorted_loads = sorted_both[dims:]
    norm_local = jnp.sum(sorted_loads * sorted_loads)
    coreg_perm = jnp.dot(
        coreg_factor, gather_chan(coreg_factor).T, precision=lax.Precision.HIGHEST
    )
    reach_runs = halo * block_runs
    window_blocks = blocks_local + 2 * halo
    widened_coords = extended(sorted_coords, "samp", 1, reach_runs)
    part_sq = jnp.sum(widened_coords * widened_coords, axis=0, keepdims=True)
    win_c = jnp.concatenate(
        [widened_coords, jnp.ones_like(part_sq), part_sq], axis=0
    ).reshape(dpad, window_blocks, block_runs).transpose(1, 0, 2)
    own_sq = jnp.sum(sorted_coords * sorted_coords, axis=0, keepdims=True)
    own_t = jnp.concatenate(
        [sorted_coords * -2.0, own_sq, jnp.ones_like(own_sq)], axis=0
    ).reshape(dpad, blocks_local, block_runs).transpose(1, 2, 0)
    begin = jnp.clip(
        block_nbrs[:, 0] - (device_pos * blocks_local - halo), 0, window_blocks - slot_limit
    ).astype(jnp.int32)
    tiles = build_tiles(begin, nbr_count.astype(jnp.int32), own_t, win_c, slot_limit)
    noise_col = noise[:, None]
    iterate = jnp.zeros_like(sorted_loads)
    remainder = sorted_loads
    direction = sorted_loads
    for iteration in range(ITERS):
        rounded = direction.astype(jnp.bfloat16)
        gathered = gather_chan(rounded)
        mixed = jnp.dot(
            coreg_perm, gathered.astype(jnp.float32), precision=lax.Precision.HIGHEST
        )
        mixed_b = mixed.astype(jnp.bfloat16)
        widened = extended(mixed_b, "samp", 1, reach_runs)
        win_v = widened.reshape(chan_local, window_blocks, block_runs).transpose(1, 0, 2)
        mapped = apply_operator(begin, win_v, tiles, direction, noise_col, 4)
        curvature = jnp.sum(direction * mapped)
        if iteration + 1 == ITERS:
            stacked = jnp.concatenate([iterate, remainder, direction, mapped], axis=0)
            unsorted = jnp.zeros_like(stacked).at[:, local_perm].set(stacked)
            iterate, remainder, direction, mapped = jnp.split(unsorted, 4, axis=0)
        if iteration == 0:
            sums = global_sum(jnp.stack([norm_local, curvature]))
            norm_now, curvature = sums[0], sums[1]
        else:
            curvature = global_sum(curvature)
        step_size = norm_now / curvature
        iterate = iterate + step_size * direction
        remainder = remainder - step_size * mapped
        if iteration + 1 < ITERS:
            norm_next = global_sum(jnp.sum(remainder * remainder))
            direction = remainder + norm_next / norm_now * direction
            norm_now = norm_next
    return (iterate, remainder)


def solution(mesh):
    return jax.shard_map(
        per_device,
        mesh=mesh,
        in_specs=(
            P("chan", "samp"),
            P(None, "samp"),
            P("chan", None),
            P("chan"),
            P("samp"),
            P("samp", None),
            P("samp"),
        ),
        out_specs=(P("chan", "samp"), P("chan", "samp")),
        check_vma=False,
    )
```

```python
import functools

import jax
import jax.numpy as jnp
from jax import lax
from jax.experimental import pallas as pl
from jax.experimental.pallas import tpu as pltpu
from jax.sharding import PartitionSpec as P

ITERS = 2
SUPPORT = 5.0
AMPLITUDE = 0.05


def tile_kernel(begin_ref, count_ref, own_ref, win_ref, out_ref, *, slots, runs):
    b = pl.program_id(0)
    start = begin_ref[b]
    count = count_ref[b]
    own = own_ref[0]
    parts = jnp.concatenate([win_ref[start + s] for s in range(slots)], axis=1)
    cross = jnp.dot(
        own * -2.0, parts, precision=lax.Precision.HIGHEST, preferred_element_type=jnp.float32
    )
    own_sq = jnp.sum(own * own, axis=1, keepdims=True)
    part_sq = jnp.sum(parts * parts, axis=0, keepdims=True)
    for s in range(slots):
        cols = slice(s * runs, (s + 1) * runs)

        @pl.when(s < count)
        def _():
            squared = jnp.maximum((own_sq + part_sq[:, cols]) + cross[:, cols], 0.0)
            radius_frac = jnp.sqrt(squared) * (1.0 / SUPPORT)
            remain = jnp.maximum(1.0 - radius_frac, 0.0)
            cubed = remain * remain * remain
            val = cubed * cubed * (6.0 * radius_frac + 1.0)
            out_ref[0, :, cols] = val.astype(out_ref.dtype)

        @pl.when(s >= count)
        def _():
            out_ref[0, :, cols] = jnp.zeros((runs, runs), out_ref.dtype)


def build_tiles(begin, count, own_t, win_c, slots):
    blocks, runs, dpad = own_t.shape
    kern = functools.partial(tile_kernel, slots=slots, runs=runs)
    return pl.pallas_call(
        kern,
        grid_spec=pltpu.PrefetchScalarGridSpec(
            num_scalar_prefetch=2,
            grid=(blocks,),
            in_specs=[
                pl.BlockSpec((1, runs, dpad), lambda b, *_: (b, 0, 0)),
                pl.BlockSpec(win_c.shape, lambda b, *_: (0, 0, 0)),
            ],
            out_specs=pl.BlockSpec((1, runs, slots * runs), lambda b, *_: (b, 0, 0)),
        ),
        out_shape=jax.ShapeDtypeStruct((blocks, runs, slots * runs), jnp.bfloat16),
    )(begin, count, own_t, win_c)


def apply_kernel(begin_ref, win_ref, tile_ref, p_ref, noise_ref, out_ref, *, per_step, slots, runs):
    g = pl.program_id(0)
    noise = noise_ref[...]
    for k in range(per_step):
        start = begin_ref[g * per_step + k]
        vals = win_ref[pl.ds(start, slots)]
        cat = jnp.concatenate([vals[s] for s in range(slots)], axis=1)
        acc = lax.dot_general(
            cat, tile_ref[k], (((1,), (1,)), ((), ())), preferred_element_type=jnp.float32
        )
        cols = slice(k * runs, (k + 1) * runs)
        out_ref[:, cols] = AMPLITUDE * acc + noise * p_ref[:, cols]


def apply_operator(begin, win_v, tiles, direction, noise_col, per_step):
    blocks, runs, width = tiles.shape
    slots = width // runs
    chans, total = direction.shape
    kern = functools.partial(apply_kernel, per_step=per_step, slots=slots, runs=runs)
    return pl.pallas_call(
        kern,
        grid_spec=pltpu.PrefetchScalarGridSpec(
            num_scalar_prefetch=1,
            grid=(blocks // per_step,),
            in_specs=[
                pl.BlockSpec(win_v.shape, lambda g, *_: (0, 0, 0)),
                pl.BlockSpec((per_step, runs, width), lambda g, *_: (g, 0, 0)),
                pl.BlockSpec((chans, per_step * runs), lambda g, *_: (0, g)),
                pl.BlockSpec((chans, 1), lambda g, *_: (0, 0)),
            ],
            out_specs=pl.BlockSpec((chans, per_step * runs), lambda g, *_: (0, g)),
        ),
        out_shape=jax.ShapeDtypeStruct((chans, total), jnp.float32),
    )(begin, win_v, tiles, direction, noise_col)


def extended(block, axis, dim, width):
    count = lax.axis_size(axis)
    forward = [(i, i + 1) for i in range(count - 1)]
    backward = [(target, source) for source, target in forward]
    low = lax.ppermute(
        lax.slice_in_dim(block, block.shape[dim] - width, None, axis=dim), axis, forward
    )
    high = lax.ppermute(lax.slice_in_dim(block, 0, width, axis=dim), axis, backward)
    return jnp.concatenate([low, block, high], axis=dim)


def global_sum(value):
    for axis in ("chan", "samp"):
        count = lax.axis_size(axis)
        step = 1
        while step < count:
            pairs = [(i, i ^ step) for i in range(count)]
            value = value + lax.ppermute(value, axis, pairs)
            step *= 2
    return value


def gather_chan(rounded):
    count = lax.axis_size("chan")
    parts = [rounded]
    for shift in range(1, count):
        pairs = [((i + shift) % count, i) for i in range(count)]
        parts.append(lax.ppermute(rounded, "chan", pairs))
    return jnp.concatenate(parts, axis=0)


def per_device(loads, coords, coreg_factor, noise, run_perm, block_nbrs, nbr_count):
    chan_local, runs_local = loads.shape
    blocks_local = nbr_count.shape[0]
    block_runs = runs_local // blocks_local
    dims = coords.shape[0]
    dpad = 8
    slot_limit = block_nbrs.shape[1]
    halo = slot_limit - 1
    device_pos = lax.axis_index("samp")
    local_perm = run_perm - device_pos * runs_local
    sorted_both = jnp.take(jnp.concatenate([coords, loads], axis=0), local_perm, axis=1)
    sorted_coords = sorted_both[:dims]
    sorted_loads = sorted_both[dims:]
    norm_local = jnp.sum(sorted_loads * sorted_loads)
    coreg_perm = jnp.dot(
        coreg_factor, gather_chan(coreg_factor).T, precision=lax.Precision.HIGHEST
    )
    reach_runs = halo * block_runs
    window_blocks = blocks_local + 2 * halo
    widened_coords = extended(sorted_coords, "samp", 1, reach_runs)
    win_c = jnp.pad(
        widened_coords.reshape(dims, window_blocks, block_runs), ((0, dpad - dims), (0, 0), (0, 0))
    ).transpose(1, 0, 2)
    own_t = jnp.pad(
        sorted_coords.reshape(dims, blocks_local, block_runs), ((0, dpad - dims), (0, 0), (0, 0))
    ).transpose(1, 2, 0)
    begin = jnp.clip(
        block_nbrs[:, 0] - (device_pos * blocks_local - halo), 0, window_blocks - slot_limit
    ).astype(jnp.int32)
    tiles = build_tiles(begin, nbr_count.astype(jnp.int32), own_t, win_c, slot_limit)
    noise_col = noise[:, None]
    iterate = jnp.zeros_like(sorted_loads)
    remainder = sorted_loads
    direction = sorted_loads
    for iteration in range(ITERS):
        rounded = direction.astype(jnp.bfloat16)
        gathered = gather_chan(rounded)
        if iteration == 0:
            tiles, gathered, coreg_perm = lax.optimization_barrier((tiles, gathered, coreg_perm))
        mixed = jnp.dot(
            coreg_perm, gathered.astype(jnp.float32), precision=lax.Precision.HIGHEST
        )
        mixed_b = mixed.astype(jnp.bfloat16)
        widened = extended(mixed_b, "samp", 1, reach_runs)
        win_v = widened.reshape(chan_local, window_blocks, block_runs).transpose(1, 0, 2)
        mapped = apply_operator(begin, win_v, tiles, direction, noise_col, 4)
        curvature = jnp.sum(direction * mapped)
        if iteration + 1 == ITERS:
            stacked = jnp.concatenate([iterate, remainder, direction, mapped], axis=0)
            unsorted = jnp.zeros_like(stacked).at[:, local_perm].set(stacked)
            iterate, remainder, direction, mapped = jnp.split(unsorted, 4, axis=0)
        if iteration == 0:
            sums = global_sum(jnp.stack([norm_local, curvature]))
            norm_now, curvature = sums[0], sums[1]
        else:
            curvature = global_sum(curvature)
        step_size = norm_now / curvature
        iterate = iterate + step_size * direction
        remainder = remainder - step_size * mapped
        if iteration + 1 < ITERS:
            norm_next = global_sum(jnp.sum(remainder * remainder))
            direction = remainder + norm_next / norm_now * direction
            norm_now = norm_next
    return (iterate, remainder)


def solution(mesh):
    return jax.shard_map(
        per_device,
        mesh=mesh,
        in_specs=(
            P("chan", "samp"),
            P(None, "samp"),
            P("chan", None),
            P("chan"),
            P("samp"),
            P("samp", None),
            P("samp"),
        ),
        out_specs=(P("chan", "samp"), P("chan", "samp")),
        check_vma=False,
    )
```

```python
import functools

import jax
import jax.numpy as jnp
from jax import lax
from jax.experimental import pallas as pl
from jax.experimental.pallas import tpu as pltpu
from jax.sharding import PartitionSpec as P

ITERS = 2
SUPPORT = 5.0
AMPLITUDE = 0.05


def tile_kernel(begin_ref, count_ref, own_ref, win_ref, out_ref, *, slots, runs):
    b = pl.program_id(0)
    start = begin_ref[b]
    count = count_ref[b]
    own = own_ref[...]
    parts = jnp.concatenate([win_ref[start + s] for s in range(slots)], axis=0)
    cross = jnp.dot(
        parts, own * -2.0, precision=lax.Precision.HIGHEST, preferred_element_type=jnp.float32
    )
    own_sq = jnp.sum(own * own, axis=0, keepdims=True)
    part_sq = jnp.sum(parts * parts, axis=1, keepdims=True)
    for s in range(slots):
        rows = slice(s * runs, (s + 1) * runs)

        @pl.when(s < count)
        def _():
            squared = jnp.maximum((own_sq + part_sq[rows]) + cross[rows], 0.0)
            radius_frac = jnp.sqrt(squared) * (1.0 / SUPPORT)
            remain = jnp.maximum(1.0 - radius_frac, 0.0)
            cubed = remain * remain * remain
            val = cubed * cubed * (6.0 * radius_frac + 1.0)
            out_ref[0, rows, :] = val.astype(out_ref.dtype)

        @pl.when(s >= count)
        def _():
            out_ref[0, rows, :] = jnp.zeros((runs, runs), out_ref.dtype)


def build_tiles(begin, count, own_c, win_c, slots):
    dpad, total = own_c.shape
    runs = win_c.shape[1]
    blocks = total // runs
    kern = functools.partial(tile_kernel, slots=slots, runs=runs)
    return pl.pallas_call(
        kern,
        grid_spec=pltpu.PrefetchScalarGridSpec(
            num_scalar_prefetch=2,
            grid=(blocks,),
            in_specs=[
                pl.BlockSpec((dpad, runs), lambda b, *_: (0, b)),
                pl.BlockSpec(win_c.shape, lambda b, *_: (0, 0, 0)),
            ],
            out_specs=pl.BlockSpec((1, slots * runs, runs), lambda b, *_: (b, 0, 0)),
        ),
        out_shape=jax.ShapeDtypeStruct((blocks, slots * runs, runs), jnp.bfloat16),
    )(begin, count, own_c, win_c)


def apply_kernel(begin_ref, win_ref, tile_ref, p_ref, noise_ref, out_ref, *, per_step, slots, runs):
    g = pl.program_id(0)
    noise = noise_ref[...]
    for k in range(per_step):
        start = begin_ref[g * per_step + k]
        vals = win_ref[pl.ds(start, slots)]
        cat = jnp.concatenate([vals[s] for s in range(slots)], axis=1)
        acc = jnp.dot(cat, tile_ref[k], preferred_element_type=jnp.float32)
        cols = slice(k * runs, (k + 1) * runs)
        out_ref[:, cols] = AMPLITUDE * acc + noise * p_ref[:, cols]


def apply_operator(begin, win_v, tiles, direction, noise_col, per_step):
    blocks, width, runs = tiles.shape
    slots = width // runs
    chans, total = direction.shape
    kern = functools.partial(apply_kernel, per_step=per_step, slots=slots, runs=runs)
    return pl.pallas_call(
        kern,
        grid_spec=pltpu.PrefetchScalarGridSpec(
            num_scalar_prefetch=1,
            grid=(blocks // per_step,),
            in_specs=[
                pl.BlockSpec(win_v.shape, lambda g, *_: (0, 0, 0)),
                pl.BlockSpec((per_step, width, runs), lambda g, *_: (g, 0, 0)),
                pl.BlockSpec((chans, per_step * runs), lambda g, *_: (0, g)),
                pl.BlockSpec((chans, 1), lambda g, *_: (0, 0)),
            ],
            out_specs=pl.BlockSpec((chans, per_step * runs), lambda g, *_: (0, g)),
        ),
        out_shape=jax.ShapeDtypeStruct((chans, total), jnp.float32),
    )(begin, win_v, tiles, direction, noise_col)


def extended(block, axis, dim, width):
    count = lax.axis_size(axis)
    forward = [(i, i + 1) for i in range(count - 1)]
    backward = [(target, source) for source, target in forward]
    low = lax.ppermute(
        lax.slice_in_dim(block, block.shape[dim] - width, None, axis=dim), axis, forward
    )
    high = lax.ppermute(lax.slice_in_dim(block, 0, width, axis=dim), axis, backward)
    return jnp.concatenate([low, block, high], axis=dim)


def global_sum(value):
    for axis in ("chan", "samp"):
        count = lax.axis_size(axis)
        step = 1
        while step < count:
            pairs = [(i, i ^ step) for i in range(count)]
            value = value + lax.ppermute(value, axis, pairs)
            step *= 2
    return value


def gather_chan(rounded):
    count = lax.axis_size("chan")
    parts = [rounded]
    for shift in range(1, count):
        pairs = [((i + shift) % count, i) for i in range(count)]
        parts.append(lax.ppermute(rounded, "chan", pairs))
    return jnp.concatenate(parts, axis=0)


def per_device(loads, coords, coreg_factor, noise, run_perm, block_nbrs, nbr_count):
    chan_local, runs_local = loads.shape
    blocks_local = nbr_count.shape[0]
    block_runs = runs_local // blocks_local
    dims = coords.shape[0]
    dpad = 8
    slot_limit = block_nbrs.shape[1]
    halo = slot_limit - 1
    device_pos = lax.axis_index("samp")
    local_perm = run_perm - device_pos * runs_local
    sorted_both = jnp.take(jnp.concatenate([coords, loads], axis=0), local_perm, axis=1)
    sorted_coords = sorted_both[:dims]
    sorted_loads = sorted_both[dims:]
    norm_local = jnp.sum(sorted_loads * sorted_loads)
    coreg_perm = jnp.dot(
        coreg_factor, gather_chan(coreg_factor).T, precision=lax.Precision.HIGHEST
    )
    reach_runs = halo * block_runs
    window_blocks = blocks_local + 2 * halo
    widened_coords = extended(sorted_coords, "samp", 1, reach_runs)
    win_c = jnp.pad(
        widened_coords.reshape(dims, window_blocks, block_runs), ((0, dpad - dims), (0, 0), (0, 0))
    ).transpose(1, 2, 0)
    own_c = jnp.pad(sorted_coords, ((0, dpad - dims), (0, 0)))
    begin = jnp.clip(
        block_nbrs[:, 0] - (device_pos * blocks_local - halo), 0, window_blocks - slot_limit
    ).astype(jnp.int32)
    tiles = build_tiles(begin, nbr_count.astype(jnp.int32), own_c, win_c, slot_limit)
    noise_col = noise[:, None]
    iterate = jnp.zeros_like(sorted_loads)
    remainder = sorted_loads
    direction = sorted_loads
    for iteration in range(ITERS):
        rounded = direction.astype(jnp.bfloat16)
        gathered = gather_chan(rounded)
        if iteration == 0:
            tiles, gathered, coreg_perm = lax.optimization_barrier((tiles, gathered, coreg_perm))
        mixed = jnp.dot(
            coreg_perm, gathered.astype(jnp.float32), precision=lax.Precision.HIGHEST
        )
        mixed_b = mixed.astype(jnp.bfloat16)
        widened = extended(mixed_b, "samp", 1, reach_runs)
        win_v = widened.reshape(chan_local, window_blocks, block_runs).transpose(1, 0, 2)
        mapped = apply_operator(begin, win_v, tiles, direction, noise_col, 4)
        curvature = jnp.sum(direction * mapped)
        if iteration + 1 == ITERS:
            stacked = jnp.concatenate([iterate, remainder, direction, mapped], axis=0)
            unsorted = jnp.zeros_like(stacked).at[:, local_perm].set(stacked)
            iterate, remainder, direction, mapped = jnp.split(unsorted, 4, axis=0)
        if iteration == 0:
            sums = global_sum(jnp.stack([norm_local, curvature]))
            norm_now, curvature = sums[0], sums[1]
        else:
            curvature = global_sum(curvature)
        step_size = norm_now / curvature
        iterate = iterate + step_size * direction
        remainder = remainder - step_size * mapped
        if iteration + 1 < ITERS:
            norm_next = global_sum(jnp.sum(remainder * remainder))
            direction = remainder + norm_next / norm_now * direction
            norm_now = norm_next
    return (iterate, remainder)


def solution(mesh):
    return jax.shard_map(
        per_device,
        mesh=mesh,
        in_specs=(
            P("chan", "samp"),
            P(None, "samp"),
            P("chan", None),
            P("chan"),
            P("samp"),
            P("samp", None),
            P("samp"),
        ),
        out_specs=(P("chan", "samp"), P("chan", "samp")),
        check_vma=False,
    )
```

```python
import functools

import jax
import jax.numpy as jnp
from jax import lax
from jax.experimental import pallas as pl
from jax.experimental.pallas import tpu as pltpu
from jax.sharding import PartitionSpec as P

ITERS = 2
SUPPORT = 5.0
AMPLITUDE = 0.05


def tile_kernel(begin_ref, count_ref, own_ref, win_ref, out_ref, *, slots, runs):
    b = pl.program_id(0)
    start = begin_ref[b]
    count = count_ref[b]
    own = own_ref[0]
    parts = jnp.concatenate([win_ref[start + s] for s in range(slots)], axis=1)
    cross = jnp.dot(
        own * -2.0, parts, precision=lax.Precision.HIGHEST, preferred_element_type=jnp.float32
    )
    own_sq = jnp.sum(own * own, axis=1, keepdims=True)
    part_sq = jnp.sum(parts * parts, axis=0, keepdims=True)
    for s in range(slots):
        cols = slice(s * runs, (s + 1) * runs)

        @pl.when(s < count)
        def _():
            squared = jnp.maximum((own_sq + part_sq[:, cols]) + cross[:, cols], 0.0)
            radius_frac = jnp.sqrt(squared) * (1.0 / SUPPORT)
            remain = jnp.maximum(1.0 - radius_frac, 0.0)
            cubed = remain * remain * remain
            val = cubed * cubed * (6.0 * radius_frac + 1.0)
            out_ref[0, :, cols] = val.astype(out_ref.dtype)

        @pl.when(s >= count)
        def _():
            out_ref[0, :, cols] = jnp.zeros((runs, runs), out_ref.dtype)


def build_tiles(begin, count, own_t, win_c, slots):
    blocks, runs, dpad = own_t.shape
    kern = functools.partial(tile_kernel, slots=slots, runs=runs)
    return pl.pallas_call(
        kern,
        grid_spec=pltpu.PrefetchScalarGridSpec(
            num_scalar_prefetch=2,
            grid=(blocks,),
            in_specs=[
                pl.BlockSpec((1, runs, dpad), lambda b, *_: (b, 0, 0)),
                pl.BlockSpec(win_c.shape, lambda b, *_: (0, 0, 0)),
            ],
            out_specs=pl.BlockSpec((1, runs, slots * runs), lambda b, *_: (b, 0, 0)),
        ),
        out_shape=jax.ShapeDtypeStruct((blocks, runs, slots * runs), jnp.bfloat16),
    )(begin, count, own_t, win_c)


def apply_kernel(begin_ref, win_ref, tile_ref, p_ref, noise_ref, out_ref, *, per_step, slots, runs):
    g = pl.program_id(0)
    noise = noise_ref[...]
    for k in range(per_step):
        start = begin_ref[g * per_step + k]
        vals = win_ref[pl.ds(start, slots)]
        cat = jnp.concatenate([vals[s] for s in range(slots)], axis=1)
        acc = lax.dot_general(
            cat, tile_ref[k], (((1,), (1,)), ((), ())), preferred_element_type=jnp.float32
        )
        cols = slice(k * runs, (k + 1) * runs)
        out_ref[:, cols] = AMPLITUDE * acc + noise * p_ref[:, cols]


def apply_operator(begin, win_v, tiles, direction, noise_col, per_step):
    blocks, runs, width = tiles.shape
    slots = width // runs
    chans, total = direction.shape
    kern = functools.partial(apply_kernel, per_step=per_step, slots=slots, runs=runs)
    return pl.pallas_call(
        kern,
        grid_spec=pltpu.PrefetchScalarGridSpec(
            num_scalar_prefetch=1,
            grid=(blocks // per_step,),
            in_specs=[
                pl.BlockSpec(win_v.shape, lambda g, *_: (0, 0, 0)),
                pl.BlockSpec((per_step, runs, width), lambda g, *_: (g, 0, 0)),
                pl.BlockSpec((chans, per_step * runs), lambda g, *_: (0, g)),
                pl.BlockSpec((chans, 1), lambda g, *_: (0, 0)),
            ],
            out_specs=pl.BlockSpec((chans, per_step * runs), lambda g, *_: (0, g)),
        ),
        out_shape=jax.ShapeDtypeStruct((chans, total), jnp.float32),
    )(begin, win_v, tiles, direction, noise_col)


def extended(block, axis, dim, width):
    count = lax.axis_size(axis)
    forward = [(i, i + 1) for i in range(count - 1)]
    backward = [(target, source) for source, target in forward]
    low = lax.ppermute(
        lax.slice_in_dim(block, block.shape[dim] - width, None, axis=dim), axis, forward
    )
    high = lax.ppermute(lax.slice_in_dim(block, 0, width, axis=dim), axis, backward)
    return jnp.concatenate([low, block, high], axis=dim)


def global_sum(value):
    for axis in ("chan", "samp"):
        count = lax.axis_size(axis)
        step = 1
        while step < count:
            pairs = [(i, i ^ step) for i in range(count)]
            value = value + lax.ppermute(value, axis, pairs)
            step *= 2
    return value


def gather_chan(rounded):
    count = lax.axis_size("chan")
    parts = [rounded]
    for shift in range(1, count):
        pairs = [((i + shift) % count, i) for i in range(count)]
        parts.append(lax.ppermute(rounded, "chan", pairs))
    return jnp.concatenate(parts, axis=0)


def per_device(loads, coords, coreg_factor, noise, run_perm, block_nbrs, nbr_count):
    chan_local, runs_local = loads.shape
    blocks_local = nbr_count.shape[0]
    block_runs = runs_local // blocks_local
    dims = coords.shape[0]
    dpad = 8
    slot_limit = block_nbrs.shape[1]
    halo = slot_limit - 1
    device_pos = lax.axis_index("samp")
    local_perm = run_perm - device_pos * runs_local
    sorted_both = jnp.take(jnp.concatenate([coords, loads], axis=0), local_perm, axis=1)
    sorted_coords = sorted_both[:dims]
    sorted_loads = sorted_both[dims:]
    norm_local = jnp.sum(sorted_loads * sorted_loads)
    coreg_perm = jnp.dot(
        coreg_factor, gather_chan(coreg_factor).T, precision=lax.Precision.HIGHEST
    )
    reach_runs = halo * block_runs
    window_blocks = blocks_local + 2 * halo
    widened_coords = extended(sorted_coords, "samp", 1, reach_runs)
    widened_coords, sorted_loads = lax.optimization_barrier((widened_coords, sorted_loads))
    win_c = jnp.pad(
        widened_coords.reshape(dims, window_blocks, block_runs), ((0, dpad - dims), (0, 0), (0, 0))
    ).transpose(1, 0, 2)
    own_t = jnp.pad(
        sorted_coords.reshape(dims, blocks_local, block_runs), ((0, dpad - dims), (0, 0), (0, 0))
    ).transpose(1, 2, 0)
    begin = jnp.clip(
        block_nbrs[:, 0] - (device_pos * blocks_local - halo), 0, window_blocks - slot_limit
    ).astype(jnp.int32)
    tiles = build_tiles(begin, nbr_count.astype(jnp.int32), own_t, win_c, slot_limit)
    noise_col = noise[:, None]
    iterate = jnp.zeros_like(sorted_loads)
    remainder = sorted_loads
    direction = sorted_loads
    for iteration in range(ITERS):
        rounded = direction.astype(jnp.bfloat16)
        gathered = gather_chan(rounded)
        if iteration == 0:
            tiles, gathered, coreg_perm = lax.optimization_barrier((tiles, gathered, coreg_perm))
        mixed = jnp.dot(
            coreg_perm, gathered.astype(jnp.float32), precision=lax.Precision.HIGHEST
        )
        mixed_b = mixed.astype(jnp.bfloat16)
        widened = extended(mixed_b, "samp", 1, reach_runs)
        win_v = widened.reshape(chan_local, window_blocks, block_runs).transpose(1, 0, 2)
        mapped = apply_operator(begin, win_v, tiles, direction, noise_col, 4)
        curvature = jnp.sum(direction * mapped)
        if iteration + 1 == ITERS:
            stacked = jnp.concatenate([iterate, remainder, direction, mapped], axis=0)
            unsorted = jnp.zeros_like(stacked).at[:, local_perm].set(stacked)
            iterate, remainder, direction, mapped = jnp.split(unsorted, 4, axis=0)
        if iteration == 0:
            sums = global_sum(jnp.stack([norm_local, curvature]))
            norm_now, curvature = sums[0], sums[1]
        else:
            curvature = global_sum(curvature)
        step_size = norm_now / curvature
        iterate = iterate + step_size * direction
        remainder = remainder - step_size * mapped
        if iteration + 1 < ITERS:
            norm_next = global_sum(jnp.sum(remainder * remainder))
            direction = remainder + norm_next / norm_now * direction
            norm_now = norm_next
    return (iterate, remainder)


def solution(mesh):
    return jax.shard_map(
        per_device,
        mesh=mesh,
        in_specs=(
            P("chan", "samp"),
            P(None, "samp"),
            P("chan", None),
            P("chan"),
            P("samp"),
            P("samp", None),
            P("samp"),
        ),
        out_specs=(P("chan", "samp"), P("chan", "samp")),
        check_vma=False,
    )
```

```python
import functools

import jax
import jax.numpy as jnp
from jax import lax
from jax.experimental import pallas as pl
from jax.experimental.pallas import tpu as pltpu
from jax.sharding import PartitionSpec as P

ITERS = 2
SUPPORT = 5.0
AMPLITUDE = 0.05


def tile_kernel(begin_ref, count_ref, own_ref, win_ref, out_ref, *, slots, runs):
    b = pl.program_id(0)
    start = begin_ref[b]
    count = count_ref[b]
    own = own_ref[0]
    parts = jnp.concatenate([win_ref[start + s] for s in range(slots)], axis=1)
    cross = jnp.dot(
        own * -2.0, parts, precision=lax.Precision.HIGHEST, preferred_element_type=jnp.float32
    )
    own_sq = jnp.sum(own * own, axis=1, keepdims=True)
    part_sq = jnp.sum(parts * parts, axis=0, keepdims=True)
    for s in range(slots):
        cols = slice(s * runs, (s + 1) * runs)

        @pl.when(s < count)
        def _():
            squared = jnp.maximum((own_sq + part_sq[:, cols]) + cross[:, cols], 0.0)
            radius_frac = jnp.sqrt(squared) * (1.0 / SUPPORT)
            remain = jnp.maximum(1.0 - radius_frac, 0.0)
            cubed = remain * remain * remain
            val = cubed * cubed * (6.0 * radius_frac + 1.0)
            out_ref[0, :, cols] = val.astype(out_ref.dtype)

        @pl.when(s >= count)
        def _():
            out_ref[0, :, cols] = jnp.zeros((runs, runs), out_ref.dtype)


def build_tiles(begin, count, own_t, win_c, slots):
    blocks, runs, dpad = own_t.shape
    kern = functools.partial(tile_kernel, slots=slots, runs=runs)
    return pl.pallas_call(
        kern,
        grid_spec=pltpu.PrefetchScalarGridSpec(
            num_scalar_prefetch=2,
            grid=(blocks,),
            in_specs=[
                pl.BlockSpec((1, runs, dpad), lambda b, *_: (b, 0, 0)),
                pl.BlockSpec(win_c.shape, lambda b, *_: (0, 0, 0)),
            ],
            out_specs=pl.BlockSpec((1, runs, slots * runs), lambda b, *_: (b, 0, 0)),
        ),
        out_shape=jax.ShapeDtypeStruct((blocks, runs, slots * runs), jnp.bfloat16),
    )(begin, count, own_t, win_c)


def apply_kernel(begin_ref, win_ref, tile_ref, p_ref, noise_ref, out_ref, *, per_step, slots, runs):
    g = pl.program_id(0)
    noise = noise_ref[...]
    for k in range(per_step):
        start = begin_ref[g * per_step + k]
        vals = win_ref[pl.ds(start, slots)]
        cat = jnp.concatenate([vals[s] for s in range(slots)], axis=1)
        acc = lax.dot_general(
            cat, tile_ref[k], (((1,), (1,)), ((), ())), preferred_element_type=jnp.float32
        )
        cols = slice(k * runs, (k + 1) * runs)
        out_ref[:, cols] = AMPLITUDE * acc + noise * p_ref[:, cols]


def apply_operator(begin, win_v, tiles, direction, noise_col, per_step):
    blocks, runs, width = tiles.shape
    slots = width // runs
    chans, total = direction.shape
    kern = functools.partial(apply_kernel, per_step=per_step, slots=slots, runs=runs)
    return pl.pallas_call(
        kern,
        grid_spec=pltpu.PrefetchScalarGridSpec(
            num_scalar_prefetch=1,
            grid=(blocks // per_step,),
            in_specs=[
                pl.BlockSpec(win_v.shape, lambda g, *_: (0, 0, 0)),
                pl.BlockSpec((per_step, runs, width), lambda g, *_: (g, 0, 0)),
                pl.BlockSpec((chans, per_step * runs), lambda g, *_: (0, g)),
                pl.BlockSpec((chans, 1), lambda g, *_: (0, 0)),
            ],
            out_specs=pl.BlockSpec((chans, per_step * runs), lambda g, *_: (0, g)),
        ),
        out_shape=jax.ShapeDtypeStruct((chans, total), jnp.float32),
    )(begin, win_v, tiles, direction, noise_col)


def extended(block, axis, dim, width):
    count = lax.axis_size(axis)
    forward = [(i, i + 1) for i in range(count - 1)]
    backward = [(target, source) for source, target in forward]
    low = lax.ppermute(
        lax.slice_in_dim(block, block.shape[dim] - width, None, axis=dim), axis, forward
    )
    high = lax.ppermute(lax.slice_in_dim(block, 0, width, axis=dim), axis, backward)
    return jnp.concatenate([low, block, high], axis=dim)


def global_sum(value):
    for axis in ("chan", "samp"):
        count = lax.axis_size(axis)
        step = 1
        while step < count:
            pairs = [(i, i ^ step) for i in range(count)]
            value = value + lax.ppermute(value, axis, pairs)
            step *= 2
    return value


def gather_chan(rounded):
    count = lax.axis_size("chan")
    parts = [rounded]
    for shift in range(1, count):
        pairs = [((i + shift) % count, i) for i in range(count)]
        parts.append(lax.ppermute(rounded, "chan", pairs))
    return jnp.concatenate(parts, axis=0)


def per_device(loads, coords, coreg_factor, noise, run_perm, block_nbrs, nbr_count):
    chan_local, runs_local = loads.shape
    blocks_local = nbr_count.shape[0]
    block_runs = runs_local // blocks_local
    dims = coords.shape[0]
    dpad = 8
    slot_limit = block_nbrs.shape[1]
    halo = slot_limit - 1
    device_pos = lax.axis_index("samp")
    local_perm = run_perm - device_pos * runs_local
    inverse_perm = jnp.zeros_like(local_perm).at[local_perm].set(
        jnp.arange(runs_local, dtype=local_perm.dtype)
    )
    sorted_both = jnp.take(jnp.concatenate([coords, loads], axis=0), local_perm, axis=1)
    sorted_coords = sorted_both[:dims]
    sorted_loads = sorted_both[dims:]
    norm_local = jnp.sum(sorted_loads * sorted_loads)
    coreg_perm = jnp.dot(
        coreg_factor, gather_chan(coreg_factor).T, precision=lax.Precision.HIGHEST
    )
    reach_runs = halo * block_runs
    window_blocks = blocks_local + 2 * halo
    widened_coords = extended(sorted_coords, "samp", 1, reach_runs)
    widened_coords, sorted_loads = lax.optimization_barrier((widened_coords, sorted_loads))
    win_c = jnp.pad(
        widened_coords.reshape(dims, window_blocks, block_runs), ((0, dpad - dims), (0, 0), (0, 0))
    ).transpose(1, 0, 2)
    own_t = jnp.pad(
        sorted_coords.reshape(dims, blocks_local, block_runs), ((0, dpad - dims), (0, 0), (0, 0))
    ).transpose(1, 2, 0)
    begin = jnp.clip(
        block_nbrs[:, 0] - (device_pos * blocks_local - halo), 0, window_blocks - slot_limit
    ).astype(jnp.int32)
    tiles = build_tiles(begin, nbr_count.astype(jnp.int32), own_t, win_c, slot_limit)
    noise_col = noise[:, None]
    iterate = jnp.zeros_like(sorted_loads)
    remainder = sorted_loads
    direction = sorted_loads
    for iteration in range(ITERS):
        rounded = direction.astype(jnp.bfloat16)
        gathered = gather_chan(rounded)
        if iteration == 0:
            tiles, gathered, coreg_perm = lax.optimization_barrier((tiles, gathered, coreg_perm))
        mixed = jnp.dot(
            coreg_perm, gathered.astype(jnp.float32), precision=lax.Precision.HIGHEST
        )
        mixed_b = mixed.astype(jnp.bfloat16)
        widened = extended(mixed_b, "samp", 1, reach_runs)
        win_v = widened.reshape(chan_local, window_blocks, block_runs).transpose(1, 0, 2)
        mapped = apply_operator(begin, win_v, tiles, direction, noise_col, 4)
        curvature = jnp.sum(direction * mapped)
        if iteration + 1 == ITERS:
            stacked = jnp.concatenate([iterate, remainder, direction, mapped], axis=0)
            unsorted = jnp.take(stacked, inverse_perm, axis=1)
            iterate, remainder, direction, mapped = jnp.split(unsorted, 4, axis=0)
        if iteration == 0:
            sums = global_sum(jnp.stack([norm_local, curvature]))
            norm_now, curvature = sums[0], sums[1]
        else:
            curvature = global_sum(curvature)
        step_size = norm_now / curvature
        iterate = iterate + step_size * direction
        remainder = remainder - step_size * mapped
        if iteration + 1 < ITERS:
            norm_next = global_sum(jnp.sum(remainder * remainder))
            direction = remainder + norm_next / norm_now * direction
            norm_now = norm_next
    return (iterate, remainder)


def solution(mesh):
    return jax.shard_map(
        per_device,
        mesh=mesh,
        in_specs=(
            P("chan", "samp"),
            P(None, "samp"),
            P("chan", None),
            P("chan"),
            P("samp"),
            P("samp", None),
            P("samp"),
        ),
        out_specs=(P("chan", "samp"), P("chan", "samp")),
        check_vma=False,
    )
```

```python
import functools

import jax
import jax.numpy as jnp
from jax import lax
from jax.experimental import pallas as pl
from jax.experimental.pallas import tpu as pltpu
from jax.sharding import PartitionSpec as P

ITERS = 2
SUPPORT = 5.0
AMPLITUDE = 0.05


def tile_kernel(begin_ref, count_ref, own_ref, win_ref, out_ref, *, slots, runs):
    b = pl.program_id(0)
    start = begin_ref[b]
    count = count_ref[b]
    own = own_ref[0]
    parts = jnp.concatenate([win_ref[start + s] for s in range(slots)], axis=1)
    cross = jnp.dot(
        own * -2.0, parts, precision=lax.Precision.HIGH, preferred_element_type=jnp.float32
    )
    own_sq = jnp.sum(own * own, axis=1, keepdims=True)
    part_sq = jnp.sum(parts * parts, axis=0, keepdims=True)
    for s in range(slots):
        cols = slice(s * runs, (s + 1) * runs)

        @pl.when(s < count)
        def _():
            squared = jnp.maximum((own_sq + part_sq[:, cols]) + cross[:, cols], 0.0)
            radius_frac = jnp.sqrt(squared) * (1.0 / SUPPORT)
            remain = jnp.maximum(1.0 - radius_frac, 0.0)
            cubed = remain * remain * remain
            val = cubed * cubed * (6.0 * radius_frac + 1.0)
            out_ref[0, :, cols] = val.astype(out_ref.dtype)

        @pl.when(s >= count)
        def _():
            out_ref[0, :, cols] = jnp.zeros((runs, runs), out_ref.dtype)


def build_tiles(begin, count, own_t, win_c, slots):
    blocks, runs, dpad = own_t.shape
    kern = functools.partial(tile_kernel, slots=slots, runs=runs)
    return pl.pallas_call(
        kern,
        grid_spec=pltpu.PrefetchScalarGridSpec(
            num_scalar_prefetch=2,
            grid=(blocks,),
            in_specs=[
                pl.BlockSpec((1, runs, dpad), lambda b, *_: (b, 0, 0)),
                pl.BlockSpec(win_c.shape, lambda b, *_: (0, 0, 0)),
            ],
            out_specs=pl.BlockSpec((1, runs, slots * runs), lambda b, *_: (b, 0, 0)),
        ),
        out_shape=jax.ShapeDtypeStruct((blocks, runs, slots * runs), jnp.bfloat16),
    )(begin, count, own_t, win_c)


def apply_kernel(begin_ref, win_ref, tile_ref, p_ref, noise_ref, out_ref, *, per_step, slots, runs):
    g = pl.program_id(0)
    noise = noise_ref[...]
    for k in range(per_step):
        start = begin_ref[g * per_step + k]
        vals = win_ref[pl.ds(start, slots)]
        cat = jnp.concatenate([vals[s] for s in range(slots)], axis=1)
        acc = lax.dot_general(
            cat, tile_ref[k], (((1,), (1,)), ((), ())), preferred_element_type=jnp.float32
        )
        cols = slice(k * runs, (k + 1) * runs)
        out_ref[:, cols] = AMPLITUDE * acc + noise * p_ref[:, cols]


def apply_operator(begin, win_v, tiles, direction, noise_col, per_step):
    blocks, runs, width = tiles.shape
    slots = width // runs
    chans, total = direction.shape
    kern = functools.partial(apply_kernel, per_step=per_step, slots=slots, runs=runs)
    return pl.pallas_call(
        kern,
        grid_spec=pltpu.PrefetchScalarGridSpec(
            num_scalar_prefetch=1,
            grid=(blocks // per_step,),
            in_specs=[
                pl.BlockSpec(win_v.shape, lambda g, *_: (0, 0, 0)),
                pl.BlockSpec((per_step, runs, width), lambda g, *_: (g, 0, 0)),
                pl.BlockSpec((chans, per_step * runs), lambda g, *_: (0, g)),
                pl.BlockSpec((chans, 1), lambda g, *_: (0, 0)),
            ],
            out_specs=pl.BlockSpec((chans, per_step * runs), lambda g, *_: (0, g)),
        ),
        out_shape=jax.ShapeDtypeStruct((chans, total), jnp.float32),
    )(begin, win_v, tiles, direction, noise_col)


def extended(block, axis, dim, width):
    count = lax.axis_size(axis)
    forward = [(i, i + 1) for i in range(count - 1)]
    backward = [(target, source) for source, target in forward]
    low = lax.ppermute(
        lax.slice_in_dim(block, block.shape[dim] - width, None, axis=dim), axis, forward
    )
    high = lax.ppermute(lax.slice_in_dim(block, 0, width, axis=dim), axis, backward)
    return jnp.concatenate([low, block, high], axis=dim)


def global_sum(value):
    for axis in ("chan", "samp"):
        count = lax.axis_size(axis)
        step = 1
        while step < count:
            pairs = [(i, i ^ step) for i in range(count)]
            value = value + lax.ppermute(value, axis, pairs)
            step *= 2
    return value


def gather_chan(rounded):
    count = lax.axis_size("chan")
    parts = [rounded]
    for shift in range(1, count):
        pairs = [((i + shift) % count, i) for i in range(count)]
        parts.append(lax.ppermute(rounded, "chan", pairs))
    return jnp.concatenate(parts, axis=0)


def per_device(loads, coords, coreg_factor, noise, run_perm, block_nbrs, nbr_count):
    chan_local, runs_local = loads.shape
    blocks_local = nbr_count.shape[0]
    block_runs = runs_local // blocks_local
    dims = coords.shape[0]
    dpad = 8
    slot_limit = block_nbrs.shape[1]
    halo = slot_limit - 1
    device_pos = lax.axis_index("samp")
    local_perm = run_perm - device_pos * runs_local
    sorted_both = jnp.take(jnp.concatenate([coords, loads], axis=0), local_perm, axis=1)
    sorted_coords = sorted_both[:dims]
    sorted_loads = sorted_both[dims:]
    norm_local = jnp.sum(sorted_loads * sorted_loads)
    coreg_perm = jnp.dot(
        coreg_factor, gather_chan(coreg_factor).T, precision=lax.Precision.HIGHEST
    )
    reach_runs = halo * block_runs
    window_blocks = blocks_local + 2 * halo
    widened_coords = extended(sorted_coords, "samp", 1, reach_runs)
    widened_coords, sorted_loads = lax.optimization_barrier((widened_coords, sorted_loads))
    win_c = jnp.pad(
        widened_coords.reshape(dims, window_blocks, block_runs), ((0, dpad - dims), (0, 0), (0, 0))
    ).transpose(1, 0, 2)
    own_t = jnp.pad(
        sorted_coords.reshape(dims, blocks_local, block_runs), ((0, dpad - dims), (0, 0), (0, 0))
    ).transpose(1, 2, 0)
    begin = jnp.clip(
        block_nbrs[:, 0] - (device_pos * blocks_local - halo), 0, window_blocks - slot_limit
    ).astype(jnp.int32)
    tiles = build_tiles(begin, nbr_count.astype(jnp.int32), own_t, win_c, slot_limit)
    noise_col = noise[:, None]
    iterate = jnp.zeros_like(sorted_loads)
    remainder = sorted_loads
    direction = sorted_loads
    for iteration in range(ITERS):
        rounded = direction.astype(jnp.bfloat16)
        gathered = gather_chan(rounded)
        if iteration == 0:
            tiles, gathered, coreg_perm = lax.optimization_barrier((tiles, gathered, coreg_perm))
        mixed = jnp.dot(
            coreg_perm, gathered.astype(jnp.float32), precision=lax.Precision.HIGHEST
        )
        mixed_b = mixed.astype(jnp.bfloat16)
        widened = extended(mixed_b, "samp", 1, reach_runs)
        win_v = widened.reshape(chan_local, window_blocks, block_runs).transpose(1, 0, 2)
        mapped = apply_operator(begin, win_v, tiles, direction, noise_col, 4)
        curvature = jnp.sum(direction * mapped)
        if iteration + 1 == ITERS:
            stacked = jnp.concatenate([iterate, remainder, direction, mapped], axis=0)
            unsorted = jnp.zeros_like(stacked).at[:, local_perm].set(stacked)
            iterate, remainder, direction, mapped = jnp.split(unsorted, 4, axis=0)
        if iteration == 0:
            sums = global_sum(jnp.stack([norm_local, curvature]))
            norm_now, curvature = sums[0], sums[1]
        else:
            curvature = global_sum(curvature)
        step_size = norm_now / curvature
        iterate = iterate + step_size * direction
        remainder = remainder - step_size * mapped
        if iteration + 1 < ITERS:
            norm_next = global_sum(jnp.sum(remainder * remainder))
            direction = remainder + norm_next / norm_now * direction
            norm_now = norm_next
    return (iterate, remainder)


def solution(mesh):
    return jax.shard_map(
        per_device,
        mesh=mesh,
        in_specs=(
            P("chan", "samp"),
            P(None, "samp"),
            P("chan", None),
            P("chan"),
            P("samp"),
            P("samp", None),
            P("samp"),
        ),
        out_specs=(P("chan", "samp"), P("chan", "samp")),
        check_vma=False,
    )
```

```python
import functools

import jax
import jax.numpy as jnp
from jax import lax
from jax.experimental import pallas as pl
from jax.experimental.pallas import tpu as pltpu
from jax.sharding import PartitionSpec as P

ITERS = 2
SUPPORT = 5.0
AMPLITUDE = 0.05


def tile_kernel(begin_ref, count_ref, own_ref, win_ref, out_ref, *, slots, runs, per_step):
    for k in range(per_step):
        b = pl.program_id(0) * per_step + k
        start = begin_ref[b]
        count = count_ref[b]
        own = own_ref[k]
        parts = jnp.concatenate([win_ref[start + s] for s in range(slots)], axis=1)
        cross = jnp.dot(
            own * -2.0, parts, precision=lax.Precision.HIGH, preferred_element_type=jnp.float32
        )
        own_sq = jnp.sum(own * own, axis=1, keepdims=True)
        part_sq = jnp.sum(parts * parts, axis=0, keepdims=True)
        for s in range(slots):
            cols = slice(s * runs, (s + 1) * runs)

            @pl.when(s < count)
            def _():
                squared = jnp.maximum((own_sq + part_sq[:, cols]) + cross[:, cols], 0.0)
                radius_frac = jnp.sqrt(squared) * (1.0 / SUPPORT)
                remain = jnp.maximum(1.0 - radius_frac, 0.0)
                cubed = remain * remain * remain
                val = cubed * cubed * (6.0 * radius_frac + 1.0)
                out_ref[k, :, cols] = val.astype(out_ref.dtype)

            @pl.when(s >= count)
            def _():
                out_ref[k, :, cols] = jnp.zeros((runs, runs), out_ref.dtype)


def build_tiles(begin, count, own_t, win_c, slots, per_step=2):
    blocks, runs, dpad = own_t.shape
    kern = functools.partial(tile_kernel, slots=slots, runs=runs, per_step=per_step)
    return pl.pallas_call(
        kern,
        grid_spec=pltpu.PrefetchScalarGridSpec(
            num_scalar_prefetch=2,
            grid=(blocks // per_step,),
            in_specs=[
                pl.BlockSpec((per_step, runs, dpad), lambda g, *_: (g, 0, 0)),
                pl.BlockSpec(win_c.shape, lambda g, *_: (0, 0, 0)),
            ],
            out_specs=pl.BlockSpec((per_step, runs, slots * runs), lambda g, *_: (g, 0, 0)),
        ),
        out_shape=jax.ShapeDtypeStruct((blocks, runs, slots * runs), jnp.bfloat16),
    )(begin, count, own_t, win_c)


def apply_kernel(begin_ref, win_ref, tile_ref, p_ref, noise_ref, out_ref, *, per_step, slots, runs):
    g = pl.program_id(0)
    noise = noise_ref[...]
    for k in range(per_step):
        start = begin_ref[g * per_step + k]
        vals = win_ref[pl.ds(start, slots)]
        cat = jnp.concatenate([vals[s] for s in range(slots)], axis=1)
        acc = lax.dot_general(
            cat, tile_ref[k], (((1,), (1,)), ((), ())), preferred_element_type=jnp.float32
        )
        cols = slice(k * runs, (k + 1) * runs)
        out_ref[:, cols] = AMPLITUDE * acc + noise * p_ref[:, cols]


def apply_operator(begin, win_v, tiles, direction, noise_col, per_step):
    blocks, runs, width = tiles.shape
    slots = width // runs
    chans, total = direction.shape
    kern = functools.partial(apply_kernel, per_step=per_step, slots=slots, runs=runs)
    return pl.pallas_call(
        kern,
        grid_spec=pltpu.PrefetchScalarGridSpec(
            num_scalar_prefetch=1,
            grid=(blocks // per_step,),
            in_specs=[
                pl.BlockSpec(win_v.shape, lambda g, *_: (0, 0, 0)),
                pl.BlockSpec((per_step, runs, width), lambda g, *_: (g, 0, 0)),
                pl.BlockSpec((chans, per_step * runs), lambda g, *_: (0, g)),
                pl.BlockSpec((chans, 1), lambda g, *_: (0, 0)),
            ],
            out_specs=pl.BlockSpec((chans, per_step * runs), lambda g, *_: (0, g)),
        ),
        out_shape=jax.ShapeDtypeStruct((chans, total), jnp.float32),
    )(begin, win_v, tiles, direction, noise_col)


def extended(block, axis, dim, width):
    count = lax.axis_size(axis)
    forward = [(i, i + 1) for i in range(count - 1)]
    backward = [(target, source) for source, target in forward]
    low = lax.ppermute(
        lax.slice_in_dim(block, block.shape[dim] - width, None, axis=dim), axis, forward
    )
    high = lax.ppermute(lax.slice_in_dim(block, 0, width, axis=dim), axis, backward)
    return jnp.concatenate([low, block, high], axis=dim)


def global_sum(value):
    for axis in ("chan", "samp"):
        count = lax.axis_size(axis)
        step = 1
        while step < count:
            pairs = [(i, i ^ step) for i in range(count)]
            value = value + lax.ppermute(value, axis, pairs)
            step *= 2
    return value


def gather_chan(rounded):
    count = lax.axis_size("chan")
    parts = [rounded]
    for shift in range(1, count):
        pairs = [((i + shift) % count, i) for i in range(count)]
        parts.append(lax.ppermute(rounded, "chan", pairs))
    return jnp.concatenate(parts, axis=0)


def per_device(loads, coords, coreg_factor, noise, run_perm, block_nbrs, nbr_count):
    chan_local, runs_local = loads.shape
    blocks_local = nbr_count.shape[0]
    block_runs = runs_local // blocks_local
    dims = coords.shape[0]
    dpad = 8
    slot_limit = block_nbrs.shape[1]
    halo = slot_limit - 1
    device_pos = lax.axis_index("samp")
    local_perm = run_perm - device_pos * runs_local
    sorted_both = jnp.take(jnp.concatenate([coords, loads], axis=0), local_perm, axis=1)
    sorted_coords = sorted_both[:dims]
    sorted_loads = sorted_both[dims:]
    norm_local = jnp.sum(sorted_loads * sorted_loads)
    coreg_perm = jnp.dot(
        coreg_factor, gather_chan(coreg_factor).T, precision=lax.Precision.HIGHEST
    )
    reach_runs = halo * block_runs
    window_blocks = blocks_local + 2 * halo
    widened_coords = extended(sorted_coords, "samp", 1, reach_runs)
    widened_coords, sorted_loads = lax.optimization_barrier((widened_coords, sorted_loads))
    win_c = jnp.pad(
        widened_coords.reshape(dims, window_blocks, block_runs), ((0, dpad - dims), (0, 0), (0, 0))
    ).transpose(1, 0, 2)
    own_t = jnp.pad(
        sorted_coords.reshape(dims, blocks_local, block_runs), ((0, dpad - dims), (0, 0), (0, 0))
    ).transpose(1, 2, 0)
    begin = jnp.clip(
        block_nbrs[:, 0] - (device_pos * blocks_local - halo), 0, window_blocks - slot_limit
    ).astype(jnp.int32)
    tiles = build_tiles(begin, nbr_count.astype(jnp.int32), own_t, win_c, slot_limit)
    noise_col = noise[:, None]
    iterate = jnp.zeros_like(sorted_loads)
    remainder = sorted_loads
    direction = sorted_loads
    for iteration in range(ITERS):
        rounded = direction.astype(jnp.bfloat16)
        gathered = gather_chan(rounded)
        if iteration == 0:
            tiles, gathered, coreg_perm = lax.optimization_barrier((tiles, gathered, coreg_perm))
        mixed = jnp.dot(
            coreg_perm, gathered.astype(jnp.float32), precision=lax.Precision.HIGHEST
        )
        mixed_b = mixed.astype(jnp.bfloat16)
        widened = extended(mixed_b, "samp", 1, reach_runs)
        win_v = widened.reshape(chan_local, window_blocks, block_runs).transpose(1, 0, 2)
        mapped = apply_operator(begin, win_v, tiles, direction, noise_col, 4)
        curvature = jnp.sum(direction * mapped)
        if iteration + 1 == ITERS:
            stacked = jnp.concatenate([iterate, remainder, direction, mapped], axis=0)
            unsorted = jnp.zeros_like(stacked).at[:, local_perm].set(stacked)
            iterate, remainder, direction, mapped = jnp.split(unsorted, 4, axis=0)
        if iteration == 0:
            sums = global_sum(jnp.stack([norm_local, curvature]))
            norm_now, curvature = sums[0], sums[1]
        else:
            curvature = global_sum(curvature)
        step_size = norm_now / curvature
        iterate = iterate + step_size * direction
        remainder = remainder - step_size * mapped
        if iteration + 1 < ITERS:
            norm_next = global_sum(jnp.sum(remainder * remainder))
            direction = remainder + norm_next / norm_now * direction
            norm_now = norm_next
    return (iterate, remainder)


def solution(mesh):
    return jax.shard_map(
        per_device,
        mesh=mesh,
        in_specs=(
            P("chan", "samp"),
            P(None, "samp"),
            P("chan", None),
            P("chan"),
            P("samp"),
            P("samp", None),
            P("samp"),
        ),
        out_specs=(P("chan", "samp"), P("chan", "samp")),
        check_vma=False,
    )
```

```python
import functools

import jax
import jax.numpy as jnp
from jax import lax
from jax.experimental import pallas as pl
from jax.experimental.pallas import tpu as pltpu
from jax.sharding import PartitionSpec as P

ITERS = 2
SUPPORT = 5.0
AMPLITUDE = 0.05


def tile_kernel(begin_ref, count_ref, own_ref, win_ref, out_ref, *, slots, runs, per_step):
    for k in range(per_step):
        b = pl.program_id(0) * per_step + k
        start = begin_ref[b]
        count = count_ref[b]
        own = own_ref[k]
        parts = jnp.concatenate([win_ref[start + s] for s in range(slots)], axis=1)
        cross = jnp.dot(
            own * -2.0, parts, precision=lax.Precision.HIGH, preferred_element_type=jnp.float32
        )
        own_sq = jnp.sum(own * own, axis=1, keepdims=True)
        part_sq = jnp.sum(parts * parts, axis=0, keepdims=True)
        for s in range(slots):
            cols = slice(s * runs, (s + 1) * runs)

            @pl.when(s < count)
            def _():
                squared = jnp.maximum((own_sq + part_sq[:, cols]) + cross[:, cols], 0.0)
                radius_frac = jnp.sqrt(squared) * (1.0 / SUPPORT)
                remain = jnp.maximum(1.0 - radius_frac, 0.0)
                cubed = remain * remain * remain
                val = cubed * cubed * (6.0 * radius_frac + 1.0)
                out_ref[k, :, cols] = val.astype(out_ref.dtype)

            @pl.when(s >= count)
            def _():
                out_ref[k, :, cols] = jnp.zeros((runs, runs), out_ref.dtype)


def build_tiles(begin, count, own_t, win_c, slots, per_step=3):
    blocks, runs, dpad = own_t.shape
    kern = functools.partial(tile_kernel, slots=slots, runs=runs, per_step=per_step)
    return pl.pallas_call(
        kern,
        grid_spec=pltpu.PrefetchScalarGridSpec(
            num_scalar_prefetch=2,
            grid=(blocks // per_step,),
            in_specs=[
                pl.BlockSpec((per_step, runs, dpad), lambda g, *_: (g, 0, 0)),
                pl.BlockSpec(win_c.shape, lambda g, *_: (0, 0, 0)),
            ],
            out_specs=pl.BlockSpec((per_step, runs, slots * runs), lambda g, *_: (g, 0, 0)),
        ),
        out_shape=jax.ShapeDtypeStruct((blocks, runs, slots * runs), jnp.bfloat16),
    )(begin, count, own_t, win_c)


def apply_kernel(begin_ref, win_ref, tile_ref, p_ref, noise_ref, out_ref, *, per_step, slots, runs):
    g = pl.program_id(0)
    noise = noise_ref[...]
    for k in range(per_step):
        start = begin_ref[g * per_step + k]
        vals = win_ref[pl.ds(start, slots)]
        cat = jnp.concatenate([vals[s] for s in range(slots)], axis=1)
        acc = lax.dot_general(
            cat, tile_ref[k], (((1,), (1,)), ((), ())), preferred_element_type=jnp.float32
        )
        cols = slice(k * runs, (k + 1) * runs)
        out_ref[:, cols] = AMPLITUDE * acc + noise * p_ref[:, cols]


def apply_operator(begin, win_v, tiles, direction, noise_col, per_step):
    blocks, runs, width = tiles.shape
    slots = width // runs
    chans, total = direction.shape
    kern = functools.partial(apply_kernel, per_step=per_step, slots=slots, runs=runs)
    return pl.pallas_call(
        kern,
        grid_spec=pltpu.PrefetchScalarGridSpec(
            num_scalar_prefetch=1,
            grid=(blocks // per_step,),
            in_specs=[
                pl.BlockSpec(win_v.shape, lambda g, *_: (0, 0, 0)),
                pl.BlockSpec((per_step, runs, width), lambda g, *_: (g, 0, 0)),
                pl.BlockSpec((chans, per_step * runs), lambda g, *_: (0, g)),
                pl.BlockSpec((chans, 1), lambda g, *_: (0, 0)),
            ],
            out_specs=pl.BlockSpec((chans, per_step * runs), lambda g, *_: (0, g)),
        ),
        out_shape=jax.ShapeDtypeStruct((chans, total), jnp.float32),
    )(begin, win_v, tiles, direction, noise_col)


def extended(block, axis, dim, width):
    count = lax.axis_size(axis)
    forward = [(i, i + 1) for i in range(count - 1)]
    backward = [(target, source) for source, target in forward]
    low = lax.ppermute(
        lax.slice_in_dim(block, block.shape[dim] - width, None, axis=dim), axis, forward
    )
    high = lax.ppermute(lax.slice_in_dim(block, 0, width, axis=dim), axis, backward)
    return jnp.concatenate([low, block, high], axis=dim)


def global_sum(value):
    for axis in ("chan", "samp"):
        count = lax.axis_size(axis)
        step = 1
        while step < count:
            pairs = [(i, i ^ step) for i in range(count)]
            value = value + lax.ppermute(value, axis, pairs)
            step *= 2
    return value


def gather_chan(rounded):
    count = lax.axis_size("chan")
    parts = [rounded]
    for shift in range(1, count):
        pairs = [((i + shift) % count, i) for i in range(count)]
        parts.append(lax.ppermute(rounded, "chan", pairs))
    return jnp.concatenate(parts, axis=0)


def per_device(loads, coords, coreg_factor, noise, run_perm, block_nbrs, nbr_count):
    chan_local, runs_local = loads.shape
    blocks_local = nbr_count.shape[0]
    block_runs = runs_local // blocks_local
    dims = coords.shape[0]
    dpad = 8
    slot_limit = block_nbrs.shape[1]
    halo = slot_limit - 1
    device_pos = lax.axis_index("samp")
    local_perm = run_perm - device_pos * runs_local
    sorted_both = jnp.take(jnp.concatenate([coords, loads], axis=0), local_perm, axis=1)
    sorted_coords = sorted_both[:dims]
    sorted_loads = sorted_both[dims:]
    norm_local = jnp.sum(sorted_loads * sorted_loads)
    coreg_perm = jnp.dot(
        coreg_factor, gather_chan(coreg_factor).T, precision=lax.Precision.HIGHEST
    )
    reach_runs = halo * block_runs
    window_blocks = blocks_local + 2 * halo
    widened_coords = extended(sorted_coords, "samp", 1, reach_runs)
    widened_coords, sorted_loads = lax.optimization_barrier((widened_coords, sorted_loads))
    win_c = jnp.pad(
        widened_coords.reshape(dims, window_blocks, block_runs), ((0, dpad - dims), (0, 0), (0, 0))
    ).transpose(1, 0, 2)
    own_t = jnp.pad(
        sorted_coords.reshape(dims, blocks_local, block_runs), ((0, dpad - dims), (0, 0), (0, 0))
    ).transpose(1, 2, 0)
    begin = jnp.clip(
        block_nbrs[:, 0] - (device_pos * blocks_local - halo), 0, window_blocks - slot_limit
    ).astype(jnp.int32)
    tiles = build_tiles(begin, nbr_count.astype(jnp.int32), own_t, win_c, slot_limit)
    noise_col = noise[:, None]
    iterate = jnp.zeros_like(sorted_loads)
    remainder = sorted_loads
    direction = sorted_loads
    for iteration in range(ITERS):
        rounded = direction.astype(jnp.bfloat16)
        gathered = gather_chan(rounded)
        if iteration == 0:
            tiles, gathered, coreg_perm = lax.optimization_barrier((tiles, gathered, coreg_perm))
        mixed = jnp.dot(
            coreg_perm, gathered.astype(jnp.float32), precision=lax.Precision.HIGHEST
        )
        mixed_b = mixed.astype(jnp.bfloat16)
        widened = extended(mixed_b, "samp", 1, reach_runs)
        win_v = widened.reshape(chan_local, window_blocks, block_runs).transpose(1, 0, 2)
        mapped = apply_operator(begin, win_v, tiles, direction, noise_col, 6)
        curvature = jnp.sum(direction * mapped)
        if iteration + 1 == ITERS:
            stacked = jnp.concatenate([iterate, remainder, direction, mapped], axis=0)
            unsorted = jnp.zeros_like(stacked).at[:, local_perm].set(stacked)
            iterate, remainder, direction, mapped = jnp.split(unsorted, 4, axis=0)
        if iteration == 0:
            sums = global_sum(jnp.stack([norm_local, curvature]))
            norm_now, curvature = sums[0], sums[1]
        else:
            curvature = global_sum(curvature)
        step_size = norm_now / curvature
        iterate = iterate + step_size * direction
        remainder = remainder - step_size * mapped
        if iteration + 1 < ITERS:
            norm_next = global_sum(jnp.sum(remainder * remainder))
            direction = remainder + norm_next / norm_now * direction
            norm_now = norm_next
    return (iterate, remainder)


def solution(mesh):
    return jax.shard_map(
        per_device,
        mesh=mesh,
        in_specs=(
            P("chan", "samp"),
            P(None, "samp"),
            P("chan", None),
            P("chan"),
            P("samp"),
            P("samp", None),
            P("samp"),
        ),
        out_specs=(P("chan", "samp"), P("chan", "samp")),
        check_vma=False,
    )
```

```python
import functools

import jax
import jax.numpy as jnp
from jax import lax
from jax.experimental import pallas as pl
from jax.experimental.pallas import tpu as pltpu
from jax.sharding import PartitionSpec as P

ITERS = 2
SUPPORT = 5.0
AMPLITUDE = 0.05


def tile_kernel(begin_ref, count_ref, own_ref, win_ref, out_ref, *, slots, runs, per_step):
    for k in range(per_step):
        b = pl.program_id(0) * per_step + k
        start = begin_ref[b]
        count = count_ref[b]
        own = own_ref[k]
        parts = jnp.concatenate([win_ref[start + s] for s in range(slots)], axis=1)
        cross = jnp.dot(
            own * -2.0, parts, precision=lax.Precision.HIGH, preferred_element_type=jnp.float32
        )
        own_sq = jnp.sum(own * own, axis=1, keepdims=True)
        part_sq = jnp.sum(parts * parts, axis=0, keepdims=True)
        for s in range(slots):
            cols = slice(s * runs, (s + 1) * runs)

            @pl.when(s < count)
            def _():
                squared = jnp.maximum((own_sq + part_sq[:, cols]) + cross[:, cols], 0.0)
                radius_frac = jnp.sqrt(squared) * (1.0 / SUPPORT)
                remain = jnp.maximum(1.0 - radius_frac, 0.0)
                cubed = remain * remain * remain
                val = cubed * cubed * (6.0 * radius_frac + 1.0)
                out_ref[k, :, cols] = val.astype(out_ref.dtype)

            @pl.when(s >= count)
            def _():
                out_ref[k, :, cols] = jnp.zeros((runs, runs), out_ref.dtype)


def build_tiles(begin, count, own_t, win_c, slots, per_step=2):
    blocks, runs, dpad = own_t.shape
    kern = functools.partial(tile_kernel, slots=slots, runs=runs, per_step=per_step)
    return pl.pallas_call(
        kern,
        grid_spec=pltpu.PrefetchScalarGridSpec(
            num_scalar_prefetch=2,
            grid=(blocks // per_step,),
            in_specs=[
                pl.BlockSpec((per_step, runs, dpad), lambda g, *_: (g, 0, 0)),
                pl.BlockSpec(win_c.shape, lambda g, *_: (0, 0, 0)),
            ],
            out_specs=pl.BlockSpec((per_step, runs, slots * runs), lambda g, *_: (g, 0, 0)),
        ),
        out_shape=jax.ShapeDtypeStruct((blocks, runs, slots * runs), jnp.bfloat16),
    )(begin, count, own_t, win_c)


def apply_kernel(begin_ref, win_ref, tile_ref, p_ref, noise_ref, out_ref, sum_ref, *, per_step, slots, runs):
    g = pl.program_id(0)
    noise = noise_ref[...]
    partial = jnp.zeros((1, runs), jnp.float32)
    for k in range(per_step):
        start = begin_ref[g * per_step + k]
        vals = win_ref[pl.ds(start, slots)]
        cat = jnp.concatenate([vals[s] for s in range(slots)], axis=1)
        acc = lax.dot_general(
            cat, tile_ref[k], (((1,), (1,)), ((), ())), preferred_element_type=jnp.float32
        )
        cols = slice(k * runs, (k + 1) * runs)
        p_blk = p_ref[:, cols]
        val = AMPLITUDE * acc + noise * p_blk
        out_ref[:, cols] = val
        partial = partial + jnp.sum(p_blk * val, axis=0, keepdims=True)
    sum_ref[...] = jnp.broadcast_to(partial, sum_ref.shape)


def apply_operator(begin, win_v, tiles, direction, noise_col, per_step):
    blocks, runs, width = tiles.shape
    slots = width // runs
    chans, total = direction.shape
    kern = functools.partial(apply_kernel, per_step=per_step, slots=slots, runs=runs)
    return pl.pallas_call(
        kern,
        grid_spec=pltpu.PrefetchScalarGridSpec(
            num_scalar_prefetch=1,
            grid=(blocks // per_step,),
            in_specs=[
                pl.BlockSpec(win_v.shape, lambda g, *_: (0, 0, 0)),
                pl.BlockSpec((per_step, runs, width), lambda g, *_: (g, 0, 0)),
                pl.BlockSpec((chans, per_step * runs), lambda g, *_: (0, g)),
                pl.BlockSpec((chans, 1), lambda g, *_: (0, 0)),
            ],
            out_specs=[
                pl.BlockSpec((chans, per_step * runs), lambda g, *_: (0, g)),
                pl.BlockSpec((1, 8, runs), lambda g, *_: (g, 0, 0)),
            ],
        ),
        out_shape=[
            jax.ShapeDtypeStruct((chans, total), jnp.float32),
            jax.ShapeDtypeStruct((blocks // per_step, 8, runs), jnp.float32),
        ],
    )(begin, win_v, tiles, direction, noise_col)


def extended(block, axis, dim, width):
    count = lax.axis_size(axis)
    forward = [(i, i + 1) for i in range(count - 1)]
    backward = [(target, source) for source, target in forward]
    low = lax.ppermute(
        lax.slice_in_dim(block, block.shape[dim] - width, None, axis=dim), axis, forward
    )
    high = lax.ppermute(lax.slice_in_dim(block, 0, width, axis=dim), axis, backward)
    return jnp.concatenate([low, block, high], axis=dim)


def global_sum(value):
    for axis in ("chan", "samp"):
        count = lax.axis_size(axis)
        step = 1
        while step < count:
            pairs = [(i, i ^ step) for i in range(count)]
            value = value + lax.ppermute(value, axis, pairs)
            step *= 2
    return value


def gather_chan(rounded):
    count = lax.axis_size("chan")
    parts = [rounded]
    for shift in range(1, count):
        pairs = [((i + shift) % count, i) for i in range(count)]
        parts.append(lax.ppermute(rounded, "chan", pairs))
    return jnp.concatenate(parts, axis=0)


def per_device(loads, coords, coreg_factor, noise, run_perm, block_nbrs, nbr_count):
    chan_local, runs_local = loads.shape
    blocks_local = nbr_count.shape[0]
    block_runs = runs_local // blocks_local
    dims = coords.shape[0]
    dpad = 8
    slot_limit = block_nbrs.shape[1]
    halo = slot_limit - 1
    device_pos = lax.axis_index("samp")
    local_perm = run_perm - device_pos * runs_local
    sorted_both = jnp.take(jnp.concatenate([coords, loads], axis=0), local_perm, axis=1)
    sorted_coords = sorted_both[:dims]
    sorted_loads = sorted_both[dims:]
    norm_local = jnp.sum(sorted_loads * sorted_loads)
    coreg_perm = jnp.dot(
        coreg_factor, gather_chan(coreg_factor).T, precision=lax.Precision.HIGHEST
    )
    reach_runs = halo * block_runs
    window_blocks = blocks_local + 2 * halo
    widened_coords = extended(sorted_coords, "samp", 1, reach_runs)
    widened_coords, sorted_loads = lax.optimization_barrier((widened_coords, sorted_loads))
    win_c = jnp.pad(
        widened_coords.reshape(dims, window_blocks, block_runs), ((0, dpad - dims), (0, 0), (0, 0))
    ).transpose(1, 0, 2)
    own_t = jnp.pad(
        sorted_coords.reshape(dims, blocks_local, block_runs), ((0, dpad - dims), (0, 0), (0, 0))
    ).transpose(1, 2, 0)
    begin = jnp.clip(
        block_nbrs[:, 0] - (device_pos * blocks_local - halo), 0, window_blocks - slot_limit
    ).astype(jnp.int32)
    tiles = build_tiles(begin, nbr_count.astype(jnp.int32), own_t, win_c, slot_limit)
    noise_col = noise[:, None]
    iterate = jnp.zeros_like(sorted_loads)
    remainder = sorted_loads
    direction = sorted_loads
    for iteration in range(ITERS):
        rounded = direction.astype(jnp.bfloat16)
        gathered = gather_chan(rounded)
        if iteration == 0:
            tiles, gathered, coreg_perm = lax.optimization_barrier((tiles, gathered, coreg_perm))
        mixed = jnp.dot(
            coreg_perm, gathered.astype(jnp.float32), precision=lax.Precision.HIGHEST
        )
        mixed_b = mixed.astype(jnp.bfloat16)
        widened = extended(mixed_b, "samp", 1, reach_runs)
        win_v = widened.reshape(chan_local, window_blocks, block_runs).transpose(1, 0, 2)
        mapped, partials = apply_operator(begin, win_v, tiles, direction, noise_col, 4)
        curvature = jnp.sum(partials[:, 0, :])
        if iteration + 1 == ITERS:
            stacked = jnp.concatenate([iterate, remainder, direction, mapped], axis=0)
            unsorted = jnp.zeros_like(stacked).at[:, local_perm].set(stacked)
            iterate, remainder, direction, mapped = jnp.split(unsorted, 4, axis=0)
        if iteration == 0:
            sums = global_sum(jnp.stack([norm_local, curvature]))
            norm_now, curvature = sums[0], sums[1]
        else:
            curvature = global_sum(curvature)
        step_size = norm_now / curvature
        iterate = iterate + step_size * direction
        remainder = remainder - step_size * mapped
        if iteration + 1 < ITERS:
            norm_next = global_sum(jnp.sum(remainder * remainder))
            direction = remainder + norm_next / norm_now * direction
            norm_now = norm_next
    return (iterate, remainder)


def solution(mesh):
    return jax.shard_map(
        per_device,
        mesh=mesh,
        in_specs=(
            P("chan", "samp"),
            P(None, "samp"),
            P("chan", None),
            P("chan"),
            P("samp"),
            P("samp", None),
            P("samp"),
        ),
        out_specs=(P("chan", "samp"), P("chan", "samp")),
        check_vma=False,
    )
```

```python
import functools

import jax
import jax.numpy as jnp
from jax import lax
from jax.experimental import pallas as pl
from jax.experimental.pallas import tpu as pltpu
from jax.sharding import PartitionSpec as P

ITERS = 2
SUPPORT = 5.0
AMPLITUDE = 0.05


def tile_kernel(begin_ref, count_ref, own_ref, win_ref, out_ref, *, slots, runs, per_step):
    for k in range(per_step):
        b = pl.program_id(0) * per_step + k
        start = begin_ref[b]
        count = count_ref[b]
        own = own_ref[k]
        parts = jnp.concatenate([win_ref[start + s] for s in range(slots)], axis=1)
        cross = jnp.dot(
            own * -2.0, parts, precision=lax.Precision.HIGH, preferred_element_type=jnp.float32
        )
        own_sq = jnp.sum(own * own, axis=1, keepdims=True)
        part_sq = jnp.sum(parts * parts, axis=0, keepdims=True)
        for s in range(slots):
            cols = slice(s * runs, (s + 1) * runs)

            @pl.when(s < count)
            def _():
                squared = jnp.maximum((own_sq + part_sq[:, cols]) + cross[:, cols], 0.0)
                radius_frac = jnp.sqrt(squared) * (1.0 / SUPPORT)
                remain = jnp.maximum(1.0 - radius_frac, 0.0)
                cubed = remain * remain * remain
                val = cubed * cubed * (6.0 * radius_frac + 1.0)
                out_ref[k, :, cols] = val.astype(out_ref.dtype)

            @pl.when(s >= count)
            def _():
                out_ref[k, :, cols] = jnp.zeros((runs, runs), out_ref.dtype)


def build_tiles(begin, count, own_t, win_c, slots, per_step=2):
    blocks, runs, dpad = own_t.shape
    kern = functools.partial(tile_kernel, slots=slots, runs=runs, per_step=per_step)
    return pl.pallas_call(
        kern,
        grid_spec=pltpu.PrefetchScalarGridSpec(
            num_scalar_prefetch=2,
            grid=(blocks // per_step,),
            in_specs=[
                pl.BlockSpec((per_step, runs, dpad), lambda g, *_: (g, 0, 0)),
                pl.BlockSpec(win_c.shape, lambda g, *_: (0, 0, 0)),
            ],
            out_specs=pl.BlockSpec((per_step, runs, slots * runs), lambda g, *_: (g, 0, 0)),
        ),
        out_shape=jax.ShapeDtypeStruct((blocks, runs, slots * runs), jnp.bfloat16),
    )(begin, count, own_t, win_c)


def apply_kernel(begin_ref, win_ref, tile_ref, p_ref, noise_ref, out_ref, sum_ref, *, per_step, slots, runs):
    g = pl.program_id(0)
    noise = noise_ref[...]
    partial = jnp.zeros((1, runs), jnp.float32)
    for k in range(per_step):
        start = begin_ref[g * per_step + k]
        vals = win_ref[pl.ds(start, slots)]
        cat = jnp.concatenate([vals[s] for s in range(slots)], axis=1)
        acc = lax.dot_general(
            cat, tile_ref[k], (((1,), (1,)), ((), ())), preferred_element_type=jnp.float32
        )
        cols = slice(k * runs, (k + 1) * runs)
        p_blk = p_ref[:, cols]
        val = AMPLITUDE * acc + noise * p_blk
        out_ref[:, cols] = val
        partial = partial + jnp.sum(p_blk * val, axis=0, keepdims=True)
    sum_ref[...] = jnp.broadcast_to(partial, sum_ref.shape)


def apply_operator(begin, win_v, tiles, direction, noise_col, per_step):
    blocks, runs, width = tiles.shape
    slots = width // runs
    chans, total = direction.shape
    kern = functools.partial(apply_kernel, per_step=per_step, slots=slots, runs=runs)
    return pl.pallas_call(
        kern,
        grid_spec=pltpu.PrefetchScalarGridSpec(
            num_scalar_prefetch=1,
            grid=(blocks // per_step,),
            in_specs=[
                pl.BlockSpec(win_v.shape, lambda g, *_: (0, 0, 0)),
                pl.BlockSpec((per_step, runs, width), lambda g, *_: (g, 0, 0)),
                pl.BlockSpec((chans, per_step * runs), lambda g, *_: (0, g)),
                pl.BlockSpec((chans, 1), lambda g, *_: (0, 0)),
            ],
            out_specs=[
                pl.BlockSpec((chans, per_step * runs), lambda g, *_: (0, g)),
                pl.BlockSpec((1, 8, runs), lambda g, *_: (g, 0, 0)),
            ],
        ),
        out_shape=[
            jax.ShapeDtypeStruct((chans, total), jnp.float32),
            jax.ShapeDtypeStruct((blocks // per_step, 8, runs), jnp.float32),
        ],
    )(begin, win_v, tiles, direction, noise_col)


def extended(block, axis, dim, width):
    count = lax.axis_size(axis)
    forward = [(i, i + 1) for i in range(count - 1)]
    backward = [(target, source) for source, target in forward]
    low = lax.ppermute(
        lax.slice_in_dim(block, block.shape[dim] - width, None, axis=dim), axis, forward
    )
    high = lax.ppermute(lax.slice_in_dim(block, 0, width, axis=dim), axis, backward)
    return jnp.concatenate([low, block, high], axis=dim)


def global_sum(value, rider=None):
    rounds = 0
    for axis in ("chan", "samp"):
        count = lax.axis_size(axis)
        step = 1
        while step < count:
            pairs = [(i, i ^ step) for i in range(count)]
            value = value + lax.ppermute(value, axis, pairs)
            step *= 2
            rounds += 1
            if rider is not None and rounds == 2:
                value, rider = lax.optimization_barrier((value, rider))
    if rider is None:
        return value
    return value, rider


def gather_chan(rounded):
    count = lax.axis_size("chan")
    parts = [rounded]
    for shift in range(1, count):
        pairs = [((i + shift) % count, i) for i in range(count)]
        parts.append(lax.ppermute(rounded, "chan", pairs))
    return jnp.concatenate(parts, axis=0)


def per_device(loads, coords, coreg_factor, noise, run_perm, block_nbrs, nbr_count):
    chan_local, runs_local = loads.shape
    blocks_local = nbr_count.shape[0]
    block_runs = runs_local // blocks_local
    dims = coords.shape[0]
    dpad = 8
    slot_limit = block_nbrs.shape[1]
    halo = slot_limit - 1
    device_pos = lax.axis_index("samp")
    local_perm = run_perm - device_pos * runs_local
    sorted_both = jnp.take(jnp.concatenate([coords, loads], axis=0), local_perm, axis=1)
    sorted_coords = sorted_both[:dims]
    sorted_loads = sorted_both[dims:]
    norm_local = jnp.sum(sorted_loads * sorted_loads)
    coreg_perm = jnp.dot(
        coreg_factor, gather_chan(coreg_factor).T, precision=lax.Precision.HIGHEST
    )
    reach_runs = halo * block_runs
    window_blocks = blocks_local + 2 * halo
    widened_coords = extended(sorted_coords, "samp", 1, reach_runs)
    widened_coords, sorted_loads = lax.optimization_barrier((widened_coords, sorted_loads))
    win_c = jnp.pad(
        widened_coords.reshape(dims, window_blocks, block_runs), ((0, dpad - dims), (0, 0), (0, 0))
    ).transpose(1, 0, 2)
    own_t = jnp.pad(
        sorted_coords.reshape(dims, blocks_local, block_runs), ((0, dpad - dims), (0, 0), (0, 0))
    ).transpose(1, 2, 0)
    begin = jnp.clip(
        block_nbrs[:, 0] - (device_pos * blocks_local - halo), 0, window_blocks - slot_limit
    ).astype(jnp.int32)
    tiles = build_tiles(begin, nbr_count.astype(jnp.int32), own_t, win_c, slot_limit)
    noise_col = noise[:, None]
    iterate = jnp.zeros_like(sorted_loads)
    remainder = sorted_loads
    direction = sorted_loads
    for iteration in range(ITERS):
        rounded = direction.astype(jnp.bfloat16)
        gathered = gather_chan(rounded)
        if iteration == 0:
            tiles, gathered, coreg_perm = lax.optimization_barrier((tiles, gathered, coreg_perm))
        mixed = jnp.dot(
            coreg_perm, gathered.astype(jnp.float32), precision=lax.Precision.HIGHEST
        )
        mixed_b = mixed.astype(jnp.bfloat16)
        widened = extended(mixed_b, "samp", 1, reach_runs)
        win_v = widened.reshape(chan_local, window_blocks, block_runs).transpose(1, 0, 2)
        mapped, partials = apply_operator(begin, win_v, tiles, direction, noise_col, 4)
        curvature = jnp.sum(partials[:, 0, :])
        if iteration + 1 == ITERS:
            stacked = jnp.concatenate([direction, mapped], axis=0)
            unsorted = jnp.zeros_like(stacked).at[:, local_perm].set(stacked)
            direction, mapped = jnp.split(unsorted, 2, axis=0)
            iterate, remainder = jnp.split(early, 2, axis=0)
        if iteration == 0:
            sums = global_sum(jnp.stack([norm_local, curvature]))
            norm_now, curvature = sums[0], sums[1]
        else:
            curvature = global_sum(curvature)
        step_size = norm_now / curvature
        iterate = iterate + step_size * direction
        remainder = remainder - step_size * mapped
        if iteration + 1 < ITERS:
            both = jnp.concatenate([iterate, remainder], axis=0)
            early = jnp.zeros_like(both).at[:, local_perm].set(both)
            norm_next, early = global_sum(jnp.sum(remainder * remainder), early)
            direction = remainder + norm_next / norm_now * direction
            norm_now = norm_next
    return (iterate, remainder)


def solution(mesh):
    return jax.shard_map(
        per_device,
        mesh=mesh,
        in_specs=(
            P("chan", "samp"),
            P(None, "samp"),
            P("chan", None),
            P("chan"),
            P("samp"),
            P("samp", None),
            P("samp"),
        ),
        out_specs=(P("chan", "samp"), P("chan", "samp")),
        check_vma=False,
    )
```

```python
import functools

import jax
import jax.numpy as jnp
from jax import lax
from jax.experimental import pallas as pl
from jax.experimental.pallas import tpu as pltpu
from jax.sharding import PartitionSpec as P

ITERS = 2
SUPPORT = 5.0
AMPLITUDE = 0.05


def tile_kernel(begin_ref, count_ref, own_ref, win_ref, out_ref, *, slots, runs, per_step):
    for k in range(per_step):
        b = pl.program_id(0) * per_step + k
        start = begin_ref[b]
        count = count_ref[b]
        own = own_ref[k]
        parts = jnp.concatenate([win_ref[start + s] for s in range(slots)], axis=1)
        cross = jnp.dot(
            own * -2.0, parts, precision=lax.Precision.HIGH, preferred_element_type=jnp.float32
        )
        own_sq = jnp.sum(own * own, axis=1, keepdims=True)
        part_sq = jnp.sum(parts * parts, axis=0, keepdims=True)
        for s in range(slots):
            cols = slice(s * runs, (s + 1) * runs)

            @pl.when(s < count)
            def _():
                squared = jnp.maximum((own_sq + part_sq[:, cols]) + cross[:, cols], 0.0)
                radius_frac = jnp.sqrt(squared) * (1.0 / SUPPORT)
                remain = jnp.maximum(1.0 - radius_frac, 0.0)
                cubed = remain * remain * remain
                val = cubed * cubed * (6.0 * radius_frac + 1.0)
                out_ref[k, :, cols] = val.astype(out_ref.dtype)

            @pl.when(s >= count)
            def _():
                out_ref[k, :, cols] = jnp.zeros((runs, runs), out_ref.dtype)


def build_tiles(begin, count, own_t, win_c, slots, per_step=2):
    blocks, runs, dpad = own_t.shape
    kern = functools.partial(tile_kernel, slots=slots, runs=runs, per_step=per_step)
    return pl.pallas_call(
        kern,
        grid_spec=pltpu.PrefetchScalarGridSpec(
            num_scalar_prefetch=2,
            grid=(blocks // per_step,),
            in_specs=[
                pl.BlockSpec((per_step, runs, dpad), lambda g, *_: (g, 0, 0)),
                pl.BlockSpec(win_c.shape, lambda g, *_: (0, 0, 0)),
            ],
            out_specs=pl.BlockSpec((per_step, runs, slots * runs), lambda g, *_: (g, 0, 0)),
        ),
        out_shape=jax.ShapeDtypeStruct((blocks, runs, slots * runs), jnp.bfloat16),
    )(begin, count, own_t, win_c)


def apply_kernel(begin_ref, win_ref, tile_ref, p_ref, noise_ref, out_ref, sum_ref, *, per_step, slots, runs):
    g = pl.program_id(0)
    noise = noise_ref[...]
    partial = jnp.zeros((1, runs), jnp.float32)
    for k in range(per_step):
        start = begin_ref[g * per_step + k]
        vals = win_ref[pl.ds(start, slots)]
        cat = jnp.concatenate([vals[s] for s in range(slots)], axis=1)
        acc = lax.dot_general(
            cat, tile_ref[k], (((1,), (1,)), ((), ())), preferred_element_type=jnp.float32
        )
        cols = slice(k * runs, (k + 1) * runs)
        p_blk = p_ref[:, cols]
        val = AMPLITUDE * acc + noise * p_blk
        out_ref[:, cols] = val
        partial = partial + jnp.sum(p_blk * val, axis=0, keepdims=True)
    sum_ref[...] = jnp.broadcast_to(partial, sum_ref.shape)


def apply_operator(begin, win_v, tiles, direction, noise_col, per_step):
    blocks, runs, width = tiles.shape
    slots = width // runs
    chans, total = direction.shape
    kern = functools.partial(apply_kernel, per_step=per_step, slots=slots, runs=runs)
    return pl.pallas_call(
        kern,
        grid_spec=pltpu.PrefetchScalarGridSpec(
            num_scalar_prefetch=1,
            grid=(blocks // per_step,),
            in_specs=[
                pl.BlockSpec(win_v.shape, lambda g, *_: (0, 0, 0)),
                pl.BlockSpec((per_step, runs, width), lambda g, *_: (g, 0, 0)),
                pl.BlockSpec((chans, per_step * runs), lambda g, *_: (0, g)),
                pl.BlockSpec((chans, 1), lambda g, *_: (0, 0)),
            ],
            out_specs=[
                pl.BlockSpec((chans, per_step * runs), lambda g, *_: (0, g)),
                pl.BlockSpec((1, 8, runs), lambda g, *_: (g, 0, 0)),
            ],
        ),
        out_shape=[
            jax.ShapeDtypeStruct((chans, total), jnp.float32),
            jax.ShapeDtypeStruct((blocks // per_step, 8, runs), jnp.float32),
        ],
    )(begin, win_v, tiles, direction, noise_col)


def extended(block, axis, dim, width):
    count = lax.axis_size(axis)
    forward = [(i, i + 1) for i in range(count - 1)]
    backward = [(target, source) for source, target in forward]
    low = lax.ppermute(
        lax.slice_in_dim(block, block.shape[dim] - width, None, axis=dim), axis, forward
    )
    high = lax.ppermute(lax.slice_in_dim(block, 0, width, axis=dim), axis, backward)
    return jnp.concatenate([low, block, high], axis=dim)


def global_sum(value):
    for axis in ("chan", "samp"):
        count = lax.axis_size(axis)
        step = 1
        while step < count:
            pairs = [(i, i ^ step) for i in range(count)]
            value = value + lax.ppermute(value, axis, pairs)
            step *= 2
    return value


def gather_chan(rounded):
    count = lax.axis_size("chan")
    parts = [rounded]
    for shift in range(1, count):
        pairs = [((i + shift) % count, i) for i in range(count)]
        parts.append(lax.ppermute(rounded, "chan", pairs))
    return jnp.concatenate(parts, axis=0)


def per_device(loads, coords, coreg_factor, noise, run_perm, block_nbrs, nbr_count):
    chan_local, runs_local = loads.shape
    blocks_local = nbr_count.shape[0]
    block_runs = runs_local // blocks_local
    dims = coords.shape[0]
    dpad = 8
    slot_limit = block_nbrs.shape[1]
    halo = slot_limit - 1
    device_pos = lax.axis_index("samp")
    local_perm = run_perm - device_pos * runs_local
    sorted_both = jnp.take(jnp.concatenate([coords, loads], axis=0), local_perm, axis=1)
    sorted_coords = sorted_both[:dims]
    sorted_loads = sorted_both[dims:]
    norm_local = jnp.sum(sorted_loads * sorted_loads)
    coreg_perm = jnp.dot(
        coreg_factor, gather_chan(coreg_factor).T, precision=lax.Precision.HIGHEST
    )
    reach_runs = halo * block_runs
    window_blocks = blocks_local + 2 * halo
    widened_coords = extended(sorted_coords, "samp", 1, reach_runs)
    widened_coords, sorted_loads = lax.optimization_barrier((widened_coords, sorted_loads))
    win_c = jnp.pad(
        widened_coords.reshape(dims, window_blocks, block_runs), ((0, dpad - dims), (0, 0), (0, 0))
    ).transpose(1, 0, 2)
    own_t = jnp.pad(
        sorted_coords.reshape(dims, blocks_local, block_runs), ((0, dpad - dims), (0, 0), (0, 0))
    ).transpose(1, 2, 0)
    begin = jnp.clip(
        block_nbrs[:, 0] - (device_pos * blocks_local - halo), 0, window_blocks - slot_limit
    ).astype(jnp.int32)
    tiles = build_tiles(begin, nbr_count.astype(jnp.int32), own_t, win_c, slot_limit)
    noise_col = noise[:, None]
    iterate = jnp.zeros_like(sorted_loads)
    remainder = sorted_loads
    direction = sorted_loads
    for iteration in range(ITERS):
        rounded = direction.astype(jnp.bfloat16)
        gathered = gather_chan(rounded)
        if iteration == 0:
            tiles, gathered, coreg_perm = lax.optimization_barrier((tiles, gathered, coreg_perm))
        mixed = jnp.dot(
            coreg_perm, gathered.astype(jnp.float32), precision=lax.Precision.HIGHEST
        )
        mixed_b = mixed.astype(jnp.bfloat16)
        widened = extended(mixed_b, "samp", 1, reach_runs)
        win_v = widened.reshape(chan_local, window_blocks, block_runs).transpose(1, 0, 2)
        mapped, partials = apply_operator(begin, win_v, tiles, direction, noise_col, 8)
        curvature = jnp.sum(partials[:, 0, :])
        if iteration + 1 == ITERS:
            stacked = jnp.concatenate([iterate, remainder, direction, mapped], axis=0)
            unsorted = jnp.zeros_like(stacked).at[:, local_perm].set(stacked)
            iterate, remainder, direction, mapped = jnp.split(unsorted, 4, axis=0)
        if iteration == 0:
            sums = global_sum(jnp.stack([norm_local, curvature]))
            norm_now, curvature = sums[0], sums[1]
        else:
            curvature = global_sum(curvature)
        step_size = norm_now / curvature
        iterate = iterate + step_size * direction
        remainder = remainder - step_size * mapped
        if iteration + 1 < ITERS:
            norm_next = global_sum(jnp.sum(remainder * remainder))
            direction = remainder + norm_next / norm_now * direction
            norm_now = norm_next
    return (iterate, remainder)


def solution(mesh):
    return jax.shard_map(
        per_device,
        mesh=mesh,
        in_specs=(
            P("chan", "samp"),
            P(None, "samp"),
            P("chan", None),
            P("chan"),
            P("samp"),
            P("samp", None),
            P("samp"),
        ),
        out_specs=(P("chan", "samp"), P("chan", "samp")),
        check_vma=False,
    )
```
